256 devices in a mesh: section: 2 (over core), req: 32 (over z, y), head: 4 (over x).
Axes of the slice: x: 4, y: 4, z: 8, core: 2. Of those that a mesh axis runs over, the one named last changes fastest.
Arguments:
- token_ids: int32 [128, 4], P('req'), may hold values from 0 to 31999
- request_order: int32 [128], replicated, may hold values from 0 to 127, each once
- window_lengths: int32 [128], replicated, may hold values from 1 to 512, as said below
- embed_table: bfloat16 [32000, 2048], P(('req', 'head')), may hold values from -6 to 6
- cache_arrived: bfloat16 [2, 128, 512, 2, 2048], P('section', None, 'req', None, 'head'), may hold values from -16 to 16
- state_arrived: float32 [2, 128, 128, 16, 128], P('section', None, 'req', 'head'), may hold values from -2 to 2
- conv_history: bfloat16 [2, 128, 3, 3, 2048], P('section', 'req', None, None, 'head'), may hold values from -6 to 6
- sink_cache: bfloat16 [2, 128, 4, 2, 2048], P('section', 'req', None, None, 'head'), may hold values from -16 to 16
- w_qkv: bfloat16 [2, 2048, 3, 2048], P('section', None, None, 'head'), may hold values from -0.125 to 0.125
- w_out: bfloat16 [2, 2048, 2048], P('section', 'head'), may hold values from -0.125 to 0.125
- w_beta: bfloat16 [2, 2048, 16], P('section', None, 'head'), may hold values from -0.125 to 0.125
- conv_taps: float32 [2, 4, 3, 2048], P('section', None, None, 'head'), may hold values from -3 to 3
- pre_gain: float32 [2, 2048], P('section'), may hold values from 0.25 to 1.75
- out_gain: float32 [2, 2048], P('section', 'head'), may hold values from 0.25 to 1.75
- score_scale_table: float32 [2, 16], P('section', 'head'), may hold values from 4 to 512
Outputs:
- layer_out: bfloat16 [2, 128, 4, 2048], P('section', 'req')
- final_state: float32 [2, 128, 128, 16, 128], P('section', 'req', None, 'head')
The draws below stay inside these ranges and needn't reach their ends.
Inputs may be any that keep to these rules, and one draw needn't show every extreme that they name: `request_order`: a permutation of the arriving requests. `window_lengths`: some request holds a full window.
All inputs are finite; a program needn't handle non-finite values.
Results may differ from the reference program's by a relative error of at most 0.025.
Values may be sent and summed in bfloat16 or wider, within the bound.
No kernel may reach another device: no remote copies, remote signals or barrier semaphores. Data moves between devices by JAX's collectives and lax.ppermute only.
A program may use at most 128 MiB of HBM per device.

```python
import math
import jax
import jax.numpy as jnp
import numpy as np
from jax import lax

D = 2048
H = 16
DH = 128
VOCAB = 32000
CONV = 4
LAYERS = 2
WIN = 512
SINKS = 4
TOK = 4
REQS = 128


def draw_window_lengths(key, part):
    first_key, second_key = jax.random.split(jax.random.fold_in(key, 11))
    drawn = jax.random.randint(first_key, (REQS,), 1, WIN + 1, dtype=jnp.int32)
    chosen = jax.random.randint(second_key, (), 0, REQS, dtype=jnp.int32)
    return jnp.where(jnp.arange(REQS, dtype=jnp.int32) == chosen, WIN, drawn).astype(jnp.int32)


def draw_score_scale_table(key, part):
    base = jax.random.uniform(jax.random.fold_in(key, 23), (LAYERS, H), jnp.float32)
    return jnp.exp(jnp.log(4.0) + base * (jnp.log(16.0) - jnp.log(4.0))).astype(jnp.float32)


def keys_and_values(key, count):
    key_part, value_part = jax.random.split(jax.random.fold_in(key, 37))
    shape = (LAYERS, REQS, count, 1, D)
    keys = jnp.clip(jax.random.normal(key_part, shape, jnp.float32), -6.0, 6.0) * DH ** (-0.5)
    values = jnp.clip(jax.random.normal(value_part, shape, jnp.float32), -6.0, 6.0) * 2.0
    return jnp.concatenate([keys, values], axis=3).astype(jnp.bfloat16)


def draw_cache_arrived(key, part):
    return keys_and_values(jax.random.fold_in(key, 41), WIN)


def draw_sink_cache(key, part):
    return keys_and_values(jax.random.fold_in(key, 43), SINKS)


def with_ends(array, key, smallest, high):
    longest = array.shape.index(max(array.shape))
    spots = []
    for shift in (0, 1):
        where = [jax.random.randint(jax.random.fold_in(key, axis), (), 0, length) for axis, length in enumerate(array.shape)]
        where[longest] = (where[longest] + shift) % array.shape[longest]
        spots.append(tuple(where))
    return array.at[spots[0]].set(smallest).at[spots[1]].set(high)


def level_of(rng, dims, cuts, low, top_value):
    loudness = 1.0
    for dim, shards_of in cuts:
        draws = jax.random.uniform(jax.random.fold_in(jax.random.fold_in(rng, 6), dim), (shards_of,), jnp.float32, low / len(cuts), top_value / len(cuts))
        loudness = loudness * jnp.repeat(jnp.exp(draws), dims[dim] // shards_of).reshape((-1,) + (1,) * (len(dims) - 1 - dim))
    return loudness


def rank_bounds(amount, skew):
    loads = [(1 << 20) // math.isqrt(rank ** skew) + 1 for rank in range(1, amount + 1)]
    spread = 1 + sum(loads) // (1 << 30)
    return np.cumsum(np.array([max(1, weight // spread) for weight in loads]))


def ranked(stream_key, shape, number_of, lean):
    listing = rank_bounds(number_of, lean)
    pick = jax.random.randint(jax.random.fold_in(stream_key, 1), shape, 0, int(listing[number_of - 1]))
    rank = jnp.searchsorted(jnp.asarray(listing, jnp.int32), pick, side="right")
    return jax.random.permutation(jax.random.fold_in(stream_key, 2), number_of)[rank].astype(jnp.int32)


def scatter_about(key, shape, width, reach, pieces=(), kind=jnp.bfloat16):
    result = jax.random.normal(key, shape, jnp.float32) * width
    if len(pieces) > 0:
        result = level_of(key, shape, pieces, -0.22, 0.18) * result
    return jnp.clip(result, min=-reach, max=reach).astype(kind)


def setup_inputs(seed: int = 0) -> dict:
    seeds = jax.random.split(jax.random.key(seed), 16)
    return {
        "token_ids": with_ends(ranked(seeds[0], (REQS, TOK), VOCAB, 2), jax.random.fold_in(seeds[0], 3), 0, VOCAB - 1).astype(jnp.int32),
        "request_order": jax.random.permutation(seeds[1], REQS).astype(jnp.int32),
        "window_lengths": draw_window_lengths(jax.random.fold_in(seeds[15], 71), 0),
        "embed_table": scatter_about(seeds[3], (VOCAB, D), 1.0, 6.0, ((0, 128),)),
        "cache_arrived": draw_cache_arrived(jax.random.fold_in(seeds[15], 71), 0),
        "state_arrived": scatter_about(seeds[5], (LAYERS, REQS, DH, H, DH), 0.3, 2.0, ((0, 2), (2, 32), (3, 4)), jnp.float32),
        "conv_history": scatter_about(seeds[6], (LAYERS, REQS, CONV - 1, 3, D), 1.0, 6.0, ((0, 2), (1, 32), (4, 4))),
        "sink_cache": draw_sink_cache(jax.random.fold_in(seeds[15], 71), 0),
        "w_qkv": scatter_about(seeds[8], (LAYERS, D, 3, D), D ** -0.5, 0.125, ((0, 2), (3, 4))),
        "w_out": scatter_about(seeds[9], (LAYERS, D, D), D ** -0.5, 0.125, ((0, 2), (1, 4))),
        "w_beta": scatter_about(seeds[10], (LAYERS, D, H), D ** -0.5, 0.125, ((0, 2), (2, 4))),
        "conv_taps": scatter_about(seeds[11], (LAYERS, CONV, 3, D), 0.5, 3.0, ((0, 2), (3, 4)), jnp.float32),
        "pre_gain": jnp.clip(1.0 + 0.15 * jax.random.normal(seeds[12], (LAYERS, D), jnp.float32), 0.25, 1.75),
        "out_gain": jnp.clip(1.0 + 0.15 * jax.random.normal(seeds[13], (LAYERS, D), jnp.float32), 0.25, 1.75),
        "score_scale_table": draw_score_scale_table(jax.random.fold_in(seeds[15], 71), 0),
    }


epsilon = 1e-06

def rms_scale(values, gain_row):
    return values * lax.rsqrt(lax.optimization_barrier(jnp.mean(values * values, axis=-1, keepdims=True)) + epsilon) * gain_row

def unit_rows(values):
    return values * lax.rsqrt(lax.optimization_barrier(jnp.sum(values * values, axis=-1, keepdims=True)) + epsilon)

def rounded(values):
    return lax.optimization_barrier(values.astype(jnp.bfloat16)).astype(jnp.float32)

def reference(token_ids, request_order, window_lengths, embed_table, cache_arrived, state_arrived, conv_history, sink_cache, w_qkv, w_out, w_beta, conv_taps, pre_gain, out_gain, score_scale_table):
    stream = embed_table[token_ids]
    lengths = window_lengths[request_order]
    row_index = jnp.arange(WIN, dtype=jnp.int32)
    new_index = jnp.arange(TOK, dtype=jnp.int32)
    outputs = []
    finals = []
    for current_layer_index in range(LAYERS):
        window_cache = cache_arrived[current_layer_index][request_order]
        stored_key_rows = window_cache[:, :, 0].astype(jnp.float32).reshape(REQS, WIN, H, DH)
        cache_values = window_cache[:, :, 1].astype(jnp.float32).reshape(REQS, WIN, H, DH)
        anchor_key_rows = sink_cache[current_layer_index][:, :, 0].astype(jnp.float32).reshape(REQS, SINKS, H, DH)
        sink_values = sink_cache[current_layer_index][:, :, 1].astype(jnp.float32).reshape(REQS, SINKS, H, DH)
        delta_state = state_arrived[current_layer_index][request_order]
        history = conv_history[current_layer_index]
        qkv_matrix = w_qkv[current_layer_index].reshape(D, 3 * D)
        conv_weights = conv_taps[current_layer_index]
        softmax_scale_factor = score_scale_table[current_layer_index]
        gain_head = out_gain[current_layer_index].reshape(H, DH)
        new_keys = jnp.zeros((REQS, TOK, H, DH), jnp.bfloat16)
        new_values = jnp.zeros((REQS, TOK, H, DH), jnp.bfloat16)
        produced = []
        for position in range(TOK):
            stream_in = stream[:, position]
            normed = rms_scale(stream_in.astype(jnp.float32), pre_gain[current_layer_index]).astype(jnp.bfloat16)
            projected = jnp.dot(normed, qkv_matrix, preferred_element_type=jnp.float32).astype(jnp.bfloat16).reshape(REQS, 3, D)
            conv_window = jnp.concatenate([history, projected[:, None]], axis=1)
            activated = jax.nn.silu(lax.optimization_barrier(jnp.sum(conv_window.astype(jnp.float32) * conv_weights[None], axis=1)))
            query_vec = unit_rows(activated[:, 0].reshape(REQS, H, DH))
            key_vec = unit_rows(activated[:, 1].reshape(REQS, H, DH))
            value_vec = activated[:, 2].reshape(REQS, H, DH)
            beta_gate = jax.nn.sigmoid(jnp.dot(normed, w_beta[current_layer_index], preferred_element_type=jnp.float32))
            predicted = jnp.einsum('skhv,shk->shv', delta_state, key_vec, precision=lax.Precision.HIGHEST)
            update = jnp.transpose(key_vec, (0, 2, 1))[:, :, :, None] * (value_vec - predicted)[:, None]
            delta_state = delta_state + beta_gate[:, None, :, None] * update
            readout = jnp.einsum('skhv,shk->shv', delta_state, query_vec, precision=lax.Precision.HIGHEST)
            query_halfwidth = rounded(query_vec)
            new_keys = new_keys.at[:, position].set(key_vec.astype(jnp.bfloat16))
            new_values = new_values.at[:, position].set(value_vec.astype(jnp.bfloat16))
            incoming_key_rows = new_keys.astype(jnp.float32)
            fresh_values = new_values.astype(jnp.float32)
            stored_score_rows = jnp.einsum('xqa,xeqa->xqe', query_halfwidth, stored_key_rows) * softmax_scale_factor[None, :, None]
            anchor_score_rows = jnp.einsum('kry,kgry->krg', query_halfwidth, anchor_key_rows) * softmax_scale_factor[None, :, None]
            incoming_score_rows = jnp.einsum('kry,kgry->krg', query_halfwidth, incoming_key_rows) * softmax_scale_factor[None, :, None]
            limit = jnp.maximum(WIN - lengths, position + 1)
            cache_mask = row_index[None, None, :] >= limit[:, None, None]
            fresh_mask = (new_index <= position)[None, None, :]
            highest = lax.optimization_barrier(jnp.max(anchor_score_rows, axis=-1))
            highest = jnp.maximum(highest, lax.optimization_barrier(jnp.max(jnp.where(cache_mask, stored_score_rows, -jnp.inf), axis=-1)))
            highest = jnp.maximum(highest, lax.optimization_barrier(jnp.max(jnp.where(fresh_mask, incoming_score_rows, -jnp.inf), axis=-1)))
            cache_weights = jnp.where(cache_mask, jnp.exp(stored_score_rows - highest[:, :, None]), 0.0)
            sink_weights = jnp.exp(anchor_score_rows - highest[:, :, None])
            fresh_weights = jnp.where(fresh_mask, jnp.exp(incoming_score_rows - highest[:, :, None]), 0.0)
            weight_sum = lax.optimization_barrier(jnp.sum(cache_weights, axis=-1)) + lax.optimization_barrier(jnp.sum(sink_weights, axis=-1)) + lax.optimization_barrier(jnp.sum(fresh_weights, axis=-1))
            numerator = jnp.einsum('shw,swhd->shd', rounded(cache_weights), cache_values)
            numerator = numerator + jnp.einsum('shj,sjhd->shd', rounded(sink_weights), sink_values)
            numerator = numerator + jnp.einsum('shj,sjhd->shd', rounded(fresh_weights), fresh_values)
            attended = numerator / weight_sum[:, :, None]
            mixed_heads = (rms_scale(readout, gain_head[None]) + attended).astype(jnp.bfloat16).reshape(REQS, D)
            mixer_out = jnp.dot(mixed_heads, w_out[current_layer_index], preferred_element_type=jnp.float32)
            stream_out = (stream_in.astype(jnp.float32) + mixer_out).astype(jnp.bfloat16)
            history = jnp.concatenate([history[:, 1:], projected[:, None]], axis=1)
            produced.append(stream_out)
        stream = jnp.stack(produced, axis=1)
        outputs.append(stream)
        finals.append(delta_state)
    return (jnp.stack(outputs), jnp.stack(finals))
```

```python
import jax
import jax.numpy as jnp
from jax import lax
from jax.sharding import PartitionSpec as P

WIN = 512


epsilon = 1e-06
negative_big = -1e30


def rms_scale(values, gain_row):
    return (
        values * lax.rsqrt(jnp.mean(values * values, axis=-1, keepdims=True) + epsilon) * gain_row
    )


def unit_rows(values):
    return values * lax.rsqrt(jnp.sum(values * values, axis=-1, keepdims=True) + epsilon)


def spread(value, axis):
    peers = lax.axis_size(axis)
    copies = jnp.broadcast_to(value[None], (peers,) + value.shape)
    return lax.all_to_all(copies, axis, 0, 0, tiled=True)


def head_sum(value):
    peers = lax.axis_size("head")
    step = 1
    while step < peers:
        pairs = [(i, i ^ step) for i in range(peers)]
        value = value + lax.ppermute(value, "head", pairs)
        step *= 2
    return value


def shards(
    token_ids,
    request_order,
    window_lengths,
    embed_table,
    cache_arrived,
    state_arrived,
    conv_history,
    sink_cache,
    w_qkv,
    w_out,
    w_beta,
    conv_taps,
    pre_gain,
    out_gain,
    score_scale_table,
):
    slot_count, token_count = token_ids.shape
    groups = lax.axis_size("req")
    heads_dev = score_scale_table.shape[1]
    width = pre_gain.shape[1]
    local_width = out_gain.shape[1]
    head_dim = local_width // heads_dev
    group_index = lax.axis_index("req")
    section_index = lax.axis_index("section")
    vocab_dev = embed_table.shape[0]
    rows = slot_count * token_count

    all_ids = spread(token_ids, "req")
    first_row = lax.axis_index(("req", "head")) * vocab_dev
    onehot = (
        all_ids.reshape(-1)[:, None] == first_row + jnp.arange(vocab_dev, dtype=jnp.int32)[None, :]
    ).astype(jnp.bfloat16)
    looked_up = jnp.dot(onehot, embed_table, preferred_element_type=jnp.float32).astype(jnp.bfloat16)
    arrived_rows = lax.all_to_all(
        looked_up.reshape(groups, rows, width), "req", 0, 0, tiled=True
    )
    partial_rows = jnp.sum(arrived_rows.astype(jnp.float32), axis=0).astype(jnp.bfloat16)
    embedded = jnp.sum(spread(partial_rows, "head").astype(jnp.float32), axis=0).astype(jnp.bfloat16)

    ordered_states = jnp.take(state_arrived[0], request_order, axis=0)
    start_state = lax.all_to_all(ordered_states, "req", 0, 1, tiled=True)

    ordered_cache = jnp.take(cache_arrived[0], request_order, axis=0)
    cache_rows = ordered_cache.shape[1]
    all_slots = ordered_cache.shape[0]
    stored_key_rows = ordered_cache[:, :, 0].reshape(all_slots, cache_rows, heads_dev, head_dim)
    cache_values = ordered_cache[:, :, 1].reshape(all_slots, cache_rows, heads_dev, head_dim)
    all_lengths = jnp.take(window_lengths, request_order)
    positions = group_index * cache_rows + jnp.arange(cache_rows, dtype=jnp.int32)
    new_index = jnp.arange(token_count, dtype=jnp.int32)
    cache_limit = jnp.maximum(WIN - all_lengths[:, None], new_index[None, :] + 1)
    cache_mask = positions[None, None, None, :] >= cache_limit[:, :, None, None]

    sink_count = sink_cache.shape[2]
    anchor_key_rows = sink_cache[0][:, :, 0].reshape(slot_count, sink_count, heads_dev, head_dim)
    sink_values = sink_cache[0][:, :, 1].reshape(slot_count, sink_count, heads_dev, head_dim)
    qkv_matrix = w_qkv[0].reshape(width, 3 * local_width)
    conv_weights = conv_taps[0]
    scale = score_scale_table[0]
    gain_head = out_gain[0].reshape(heads_dev, head_dim)
    history = conv_history[0]
    fresh_mask = (new_index[None, :] <= new_index[:, None])[None, :, None, :]

    def layer(stream):
        normed = rms_scale(stream.astype(jnp.float32), pre_gain[0]).astype(jnp.bfloat16)
        projected = (
            jnp.dot(normed, qkv_matrix, preferred_element_type=jnp.float32)
            .astype(jnp.bfloat16)
            .reshape(slot_count, token_count, 3, local_width)
        )
        sequence = jnp.concatenate([history, projected], axis=1).astype(jnp.float32)
        taps = conv_weights.shape[0]
        mixed_rows = sum(
            sequence[:, i : i + token_count] * conv_weights[i][None, None] for i in range(taps)
        )
        activated = jax.nn.silu(mixed_rows)
        query_vec = unit_rows(activated[:, :, 0].reshape(slot_count, token_count, heads_dev, head_dim))
        key_vec = unit_rows(activated[:, :, 1].reshape(slot_count, token_count, heads_dev, head_dim))
        value_vec = activated[:, :, 2].reshape(slot_count, token_count, heads_dev, head_dim)
        beta_gate = jax.nn.sigmoid(
            jnp.dot(normed, w_beta[0], preferred_element_type=jnp.float32)
        ).reshape(slot_count, token_count, heads_dev)

        query_halfwidth = query_vec.astype(jnp.bfloat16)
        all_queries = spread(query_halfwidth, "req").reshape(
            all_slots, token_count, heads_dev, head_dim
        )
        stored_scores = (
            jnp.einsum(
                "rthd,rwhd->rthw",
                all_queries,
                stored_key_rows,
                preferred_element_type=jnp.float32,
            )
            * scale[None, None, :, None]
        )
        local_max = jnp.max(jnp.where(cache_mask, stored_scores, negative_big), axis=-1)
        local_weights = jnp.where(cache_mask, jnp.exp(stored_scores - local_max[..., None]), 0.0)
        local_sum = jnp.sum(local_weights, axis=-1)
        local_part = jnp.einsum(
            "rthw,rwhd->rthd",
            local_weights.astype(jnp.bfloat16),
            cache_values,
            preferred_element_type=jnp.float32,
        )
        packed = jnp.concatenate(
            [local_part, local_sum[..., None], local_max[..., None]], axis=-1
        ).reshape(groups, slot_count, token_count, heads_dev, head_dim + 2)
        gathered = lax.all_to_all(packed, "req", 0, 0, tiled=True)
        part_numer = gathered[..., :head_dim]
        part_sum = gathered[..., head_dim]
        part_max = gathered[..., head_dim + 1]

        delta_state = start_state
        readouts = []
        for t in range(token_count):
            k_t = key_vec[:, t]
            predicted = jnp.einsum(
                "skhv,shk->shv", delta_state, k_t, precision=lax.Precision.HIGHEST
            )
            update = jnp.transpose(k_t, (0, 2, 1))[:, :, :, None] * (
                value_vec[:, t] - predicted
            )[:, None]
            delta_state = delta_state + beta_gate[:, t][:, None, :, None] * update
            readouts.append(
                jnp.einsum(
                    "skhv,shk->shv", delta_state, query_vec[:, t], precision=lax.Precision.HIGHEST
                )
            )
        readout = jnp.stack(readouts, axis=1)

        new_keys = key_vec.astype(jnp.bfloat16)
        new_values = value_vec.astype(jnp.bfloat16)
        anchor_scores = (
            jnp.einsum(
                "sthd,sjhd->sthj", query_halfwidth, anchor_key_rows, preferred_element_type=jnp.float32
            )
            * scale[None, None, :, None]
        )
        incoming_scores = (
            jnp.einsum(
                "sthd,suhd->sthu", query_halfwidth, new_keys, preferred_element_type=jnp.float32
            )
            * scale[None, None, :, None]
        )
        highest = jnp.maximum(
            jnp.max(anchor_scores, axis=-1),
            jnp.max(jnp.where(fresh_mask, incoming_scores, negative_big), axis=-1),
        )
        highest = jnp.maximum(highest, jnp.max(part_max, axis=0))
        part_scale = jnp.exp(part_max - highest[None])
        sink_weights = jnp.exp(anchor_scores - highest[..., None])
        fresh_weights = jnp.where(fresh_mask, jnp.exp(incoming_scores - highest[..., None]), 0.0)
        weight_sum = (
            jnp.sum(part_scale * part_sum, axis=0)
            + jnp.sum(sink_weights, axis=-1)
            + jnp.sum(fresh_weights, axis=-1)
        )
        numerator = jnp.sum(part_scale[..., None] * part_numer, axis=0)
        numerator = numerator + jnp.einsum(
            "sthj,sjhd->sthd",
            sink_weights.astype(jnp.bfloat16),
            sink_values,
            preferred_element_type=jnp.float32,
        )
        numerator = numerator + jnp.einsum(
            "sthu,suhd->sthd",
            fresh_weights.astype(jnp.bfloat16),
            new_values,
            preferred_element_type=jnp.float32,
        )
        attended = numerator / weight_sum[..., None]
        mixed_heads = (
            (rms_scale(readout, gain_head[None, None]) + attended)
            .astype(jnp.bfloat16)
            .reshape(rows, local_width)
        )
        partial_out = jnp.dot(mixed_heads, w_out[0], preferred_element_type=jnp.float32)
        mixer_out = head_sum(partial_out)
        stream_out = (stream.astype(jnp.float32) + mixer_out).astype(jnp.bfloat16)
        return stream_out, delta_state

    first_out, first_state = layer(embedded)
    received = lax.ppermute(first_out, "section", [(0, 1)])
    second_out, second_state = layer(received)
    is_first = section_index == 0
    produced = jnp.where(is_first, first_out, second_out).reshape(slot_count, token_count, width)
    final_state = jnp.where(is_first, first_state, second_state)
    return (produced[None], final_state[None])


def solution(mesh):
    return jax.shard_map(
        shards,
        mesh=mesh,
        in_specs=(
            P("req", None),
            P(),
            P(),
            P(("req", "head"), None),
            P("section", None, "req", None, "head"),
            P("section", None, "req", "head", None),
            P("section", "req", None, None, "head"),
            P("section", "req", None, None, "head"),
            P("section", None, None, "head"),
            P("section", "head", None),
            P("section", None, "head"),
            P("section", None, None, "head"),
            P("section", None),
            P("section", "head"),
            P("section", "head"),
        ),
        out_specs=(P("section", "req", None, None), P("section", "req", None, "head", None)),
        check_vma=False,
    )
```

```python
import jax
import jax.numpy as jnp
from jax import lax
from jax.sharding import PartitionSpec as P

WIN = 512


epsilon = 1e-06
negative_big = -1e30


def rms_scale(values, gain_row):
    return (
        values * lax.rsqrt(jnp.mean(values * values, axis=-1, keepdims=True) + epsilon) * gain_row
    )


def unit_rows(values):
    return values * lax.rsqrt(jnp.sum(values * values, axis=-1, keepdims=True) + epsilon)


def spread(value, axis):
    peers = lax.axis_size(axis)
    copies = jnp.broadcast_to(value[None], (peers,) + value.shape)
    return lax.all_to_all(copies, axis, 0, 0, tiled=True)


def head_sum(value):
    peers = lax.axis_size("head")
    step = 1
    while step < peers:
        pairs = [(i, i ^ step) for i in range(peers)]
        value = value + lax.ppermute(value, "head", pairs)
        step *= 2
    return value


def shards(
    token_ids,
    request_order,
    window_lengths,
    embed_table,
    cache_arrived,
    state_arrived,
    conv_history,
    sink_cache,
    w_qkv,
    w_out,
    w_beta,
    conv_taps,
    pre_gain,
    out_gain,
    score_scale_table,
):
    slot_count, token_count = token_ids.shape
    groups = lax.axis_size("req")
    heads_dev = score_scale_table.shape[1]
    width = pre_gain.shape[1]
    local_width = out_gain.shape[1]
    head_dim = local_width // heads_dev
    group_index = lax.axis_index("req")
    section_index = lax.axis_index("section")
    vocab_dev = embed_table.shape[0]
    rows = slot_count * token_count

    all_ids = spread(token_ids, "req")
    first_row = lax.axis_index(("req", "head")) * vocab_dev
    onehot = (
        all_ids.reshape(-1)[:, None] == first_row + jnp.arange(vocab_dev, dtype=jnp.int32)[None, :]
    ).astype(jnp.bfloat16)
    looked_up = jnp.dot(onehot, embed_table, preferred_element_type=jnp.float32).astype(jnp.bfloat16)
    arrived_rows = lax.all_to_all(
        looked_up.reshape(groups, rows, width), "req", 0, 0, tiled=True
    )
    partial_rows = jnp.sum(arrived_rows.astype(jnp.float32), axis=0).astype(jnp.bfloat16)
    embedded = jnp.sum(spread(partial_rows, "head").astype(jnp.float32), axis=0).astype(jnp.bfloat16)

    ordered_states = jnp.take(state_arrived[0], request_order, axis=0)
    start_state = lax.all_to_all(ordered_states, "req", 0, 1, tiled=True)

    ordered_cache = jnp.take(cache_arrived[0], request_order, axis=0)
    cache_rows = ordered_cache.shape[1]
    all_slots = ordered_cache.shape[0]
    stored_key_rows = ordered_cache[:, :, 0].reshape(all_slots, cache_rows, heads_dev, head_dim)
    cache_values = ordered_cache[:, :, 1].reshape(all_slots, cache_rows, heads_dev, head_dim)
    all_lengths = jnp.take(window_lengths, request_order)
    positions = group_index * cache_rows + jnp.arange(cache_rows, dtype=jnp.int32)
    new_index = jnp.arange(token_count, dtype=jnp.int32)
    cache_limit = jnp.maximum(WIN - all_lengths[:, None], new_index[None, :] + 1)
    cache_mask = positions[None, None, None, :] >= cache_limit[:, :, None, None]

    sink_count = sink_cache.shape[2]
    anchor_key_rows = sink_cache[0][:, :, 0].reshape(slot_count, sink_count, heads_dev, head_dim)
    sink_values = sink_cache[0][:, :, 1].reshape(slot_count, sink_count, heads_dev, head_dim)
    qkv_matrix = w_qkv[0].reshape(width, 3 * local_width)
    conv_weights = conv_taps[0]
    scale = score_scale_table[0]
    gain_head = out_gain[0].reshape(heads_dev, head_dim)
    history = conv_history[0]
    fresh_mask = (new_index[None, :] <= new_index[:, None])[None, :, None, :]

    def layer(stream):
        normed = rms_scale(stream.astype(jnp.float32), pre_gain[0]).astype(jnp.bfloat16)
        projected = (
            jnp.dot(normed, qkv_matrix, preferred_element_type=jnp.float32)
            .astype(jnp.bfloat16)
            .reshape(slot_count, token_count, 3, local_width)
        )
        sequence = jnp.concatenate([history, projected], axis=1).astype(jnp.float32)
        taps = conv_weights.shape[0]
        mixed_rows = sum(
            sequence[:, i : i + token_count] * conv_weights[i][None, None] for i in range(taps)
        )
        activated = jax.nn.silu(mixed_rows)
        query_vec = unit_rows(activated[:, :, 0].reshape(slot_count, token_count, heads_dev, head_dim))
        key_vec = unit_rows(activated[:, :, 1].reshape(slot_count, token_count, heads_dev, head_dim))
        value_vec = activated[:, :, 2].reshape(slot_count, token_count, heads_dev, head_dim)
        beta_gate = jax.nn.sigmoid(
            jnp.dot(normed, w_beta[0], preferred_element_type=jnp.float32)
        ).reshape(slot_count, token_count, heads_dev)

        query_halfwidth = query_vec.astype(jnp.bfloat16)
        all_queries = spread(query_halfwidth, "req").reshape(
            all_slots, token_count, heads_dev, head_dim
        )
        stored_scores = (
            jnp.einsum(
                "rthd,rwhd->rthw",
                all_queries,
                stored_key_rows,
                preferred_element_type=jnp.float32,
            )
            * scale[None, None, :, None]
        )
        local_max = jnp.max(jnp.where(cache_mask, stored_scores, negative_big), axis=-1)
        local_weights = jnp.where(cache_mask, jnp.exp(stored_scores - local_max[..., None]), 0.0)
        local_sum = jnp.sum(local_weights, axis=-1)
        local_part = jnp.einsum(
            "rthw,rwhd->rthd",
            local_weights.astype(jnp.bfloat16),
            cache_values,
            preferred_element_type=jnp.float32,
        )
        stats = jnp.concatenate(
            [
                local_sum,
                local_max,
                jnp.zeros((all_slots, token_count, head_dim - 2 * heads_dev), jnp.float32),
            ],
            axis=-1,
        )
        packed = jnp.concatenate([local_part, stats[:, :, None, :]], axis=2).reshape(
            groups, slot_count, token_count, heads_dev + 1, head_dim
        )
        gathered = lax.all_to_all(packed, "req", 0, 0, tiled=True)
        part_numer = gathered[:, :, :, :heads_dev]
        part_sum = gathered[:, :, :, heads_dev, :heads_dev]
        part_max = gathered[:, :, :, heads_dev, heads_dev : 2 * heads_dev]

        delta_state = start_state
        readouts = []
        for t in range(token_count):
            k_t = jnp.transpose(key_vec[:, t], (0, 2, 1))[:, :, :, None]
            q_t = jnp.transpose(query_vec[:, t], (0, 2, 1))[:, :, :, None]
            predicted = jnp.sum(delta_state * k_t, axis=1)
            update = k_t * (value_vec[:, t] - predicted)[:, None]
            delta_state = delta_state + beta_gate[:, t][:, None, :, None] * update
            readouts.append(jnp.sum(delta_state * q_t, axis=1))
        readout = jnp.stack(readouts, axis=1)

        new_keys = key_vec.astype(jnp.bfloat16)
        new_values = value_vec.astype(jnp.bfloat16)
        anchor_scores = (
            jnp.einsum(
                "sthd,sjhd->sthj", query_halfwidth, anchor_key_rows, preferred_element_type=jnp.float32
            )
            * scale[None, None, :, None]
        )
        incoming_scores = (
            jnp.einsum(
                "sthd,suhd->sthu", query_halfwidth, new_keys, preferred_element_type=jnp.float32
            )
            * scale[None, None, :, None]
        )
        highest = jnp.maximum(
            jnp.max(anchor_scores, axis=-1),
            jnp.max(jnp.where(fresh_mask, incoming_scores, negative_big), axis=-1),
        )
        highest = jnp.maximum(highest, jnp.max(part_max, axis=0))
        part_scale = jnp.exp(part_max - highest[None])
        sink_weights = jnp.exp(anchor_scores - highest[..., None])
        fresh_weights = jnp.where(fresh_mask, jnp.exp(incoming_scores - highest[..., None]), 0.0)
        weight_sum = (
            jnp.sum(part_scale * part_sum, axis=0)
            + jnp.sum(sink_weights, axis=-1)
            + jnp.sum(fresh_weights, axis=-1)
        )
        numerator = jnp.sum(part_scale[..., None] * part_numer, axis=0)
        numerator = numerator + jnp.einsum(
            "sthj,sjhd->sthd",
            sink_weights.astype(jnp.bfloat16),
            sink_values,
            preferred_element_type=jnp.float32,
        )
        numerator = numerator + jnp.einsum(
            "sthu,suhd->sthd",
            fresh_weights.astype(jnp.bfloat16),
            new_values,
            preferred_element_type=jnp.float32,
        )
        attended = numerator / weight_sum[..., None]
        mixed_heads = (
            (rms_scale(readout, gain_head[None, None]) + attended)
            .astype(jnp.bfloat16)
            .reshape(rows, local_width)
        )
        partial_out = jnp.dot(mixed_heads, w_out[0], preferred_element_type=jnp.float32)
        mixer_out = head_sum(partial_out)
        stream_out = (stream.astype(jnp.float32) + mixer_out).astype(jnp.bfloat16)
        return stream_out, delta_state

    first_out, first_state = layer(embedded)
    received = lax.ppermute(first_out, "section", [(0, 1)])
    second_out, second_state = layer(received)
    is_first = section_index == 0
    produced = jnp.where(is_first, first_out, second_out).reshape(slot_count, token_count, width)
    final_state = jnp.where(is_first, first_state, second_state)
    return (produced[None], final_state[None])


def solution(mesh):
    return jax.shard_map(
        shards,
        mesh=mesh,
        in_specs=(
            P("req", None),
            P(),
            P(),
            P(("req", "head"), None),
            P("section", None, "req", None, "head"),
            P("section", None, "req", "head", None),
            P("section", "req", None, None, "head"),
            P("section", "req", None, None, "head"),
            P("section", None, None, "head"),
            P("section", "head", None),
            P("section", None, "head"),
            P("section", None, None, "head"),
            P("section", None),
            P("section", "head"),
            P("section", "head"),
        ),
        out_specs=(P("section", "req", None, None), P("section", "req", None, "head", None)),
        check_vma=False,
    )
```

```python
import jax
import jax.numpy as jnp
from jax import lax
from jax.experimental import pallas as pl
from jax.experimental.pallas import tpu as pltpu
from jax.sharding import PartitionSpec as P

WIN = 512


epsilon = 1e-06
negative_big = -1e30


def rms_scale(values, gain_row):
    return (
        values * lax.rsqrt(jnp.mean(values * values, axis=-1, keepdims=True) + epsilon) * gain_row
    )


def unit_rows(values):
    return values * lax.rsqrt(jnp.sum(values * values, axis=-1, keepdims=True) + epsilon)


def spread(value, axis):
    peers = lax.axis_size(axis)
    copies = jnp.broadcast_to(value[None], (peers,) + value.shape)
    return lax.all_to_all(copies, axis, 0, 0, tiled=True)


def head_sum(value):
    peers = lax.axis_size("head")
    step = 1
    while step < peers:
        pairs = [(i, i ^ step) for i in range(peers)]
        value = value + lax.ppermute(value, "head", pairs)
        step *= 2
    return value


def delta_rule_kernel(beta_ref, state_ref, key_ref, query_ref, value_ref, state_out, read_out):
    slots, key_rows, _ = state_ref.shape
    heads = key_ref.shape[1]
    tokens = value_ref.shape[1]
    for s in range(slots):
        for h in range(heads):
            cols = pl.ds(h * key_rows, key_rows)
            matrix = state_ref[s, :, cols]
            key_cols = key_ref[s, h]
            query_cols = query_ref[s, h]
            for t in range(tokens):
                k_t = key_cols[:, t : t + 1]
                predicted = jnp.sum(matrix * k_t, axis=0, keepdims=True)
                v_t = value_ref[s, pl.ds(t, 1), cols]
                gate = beta_ref[(s * tokens + t) * heads + h]
                matrix = matrix + gate * (k_t * (v_t - predicted))
                read_out[s, pl.ds(t, 1), cols] = jnp.sum(
                    matrix * query_cols[:, t : t + 1], axis=0, keepdims=True
                )
            state_out[s, :, cols] = matrix


def delta_rule(start_state, key_vec, query_vec, value_vec, beta_gate):
    slots, key_rows, heads, value_cols = start_state.shape
    tokens = key_vec.shape[1]
    vmem = pl.BlockSpec(memory_space=pltpu.VMEM)
    new_state, readout = pl.pallas_call(
        delta_rule_kernel,
        out_shape=(
            jax.ShapeDtypeStruct((slots, key_rows, heads * value_cols), jnp.float32),
            jax.ShapeDtypeStruct((slots, tokens, heads * value_cols), jnp.float32),
        ),
        in_specs=[pl.BlockSpec(memory_space=pltpu.SMEM), vmem, vmem, vmem, vmem],
        out_specs=(vmem, vmem),
        cost_estimate=pl.CostEstimate(
            flops=8 * slots * heads * tokens * key_rows * value_cols,
            bytes_accessed=8 * slots * key_rows * heads * value_cols,
            transcendentals=0,
        ),
    )(
        beta_gate.reshape(-1),
        start_state.reshape(slots, key_rows, heads * value_cols),
        jnp.transpose(key_vec, (0, 2, 3, 1)),
        jnp.transpose(query_vec, (0, 2, 3, 1)),
        value_vec.reshape(slots, tokens, heads * value_cols),
    )
    return (
        new_state.reshape(slots, key_rows, heads, value_cols),
        readout.reshape(slots, tokens, heads, value_cols),
    )


def shards(
    token_ids,
    request_order,
    window_lengths,
    embed_table,
    cache_arrived,
    state_arrived,
    conv_history,
    sink_cache,
    w_qkv,
    w_out,
    w_beta,
    conv_taps,
    pre_gain,
    out_gain,
    score_scale_table,
):
    slot_count, token_count = token_ids.shape
    groups = lax.axis_size("req")
    heads_dev = score_scale_table.shape[1]
    width = pre_gain.shape[1]
    local_width = out_gain.shape[1]
    head_dim = local_width // heads_dev
    group_index = lax.axis_index("req")
    section_index = lax.axis_index("section")
    vocab_dev = embed_table.shape[0]
    rows = slot_count * token_count

    all_ids = spread(token_ids, "req")
    first_row = lax.axis_index(("req", "head")) * vocab_dev
    onehot = (
        all_ids.reshape(-1)[:, None] == first_row + jnp.arange(vocab_dev, dtype=jnp.int32)[None, :]
    ).astype(jnp.bfloat16)
    looked_up = jnp.dot(onehot, embed_table, preferred_element_type=jnp.float32).astype(jnp.bfloat16)
    arrived_rows = lax.all_to_all(
        looked_up.reshape(groups, rows, width), "req", 0, 0, tiled=True
    )
    partial_rows = jnp.sum(arrived_rows.astype(jnp.float32), axis=0).astype(jnp.bfloat16)
    embedded = jnp.sum(spread(partial_rows, "head").astype(jnp.float32), axis=0).astype(jnp.bfloat16)

    ordered_states = jnp.take(state_arrived[0], request_order, axis=0)
    start_state = lax.all_to_all(ordered_states, "req", 0, 1, tiled=True)

    ordered_cache = jnp.take(cache_arrived[0], request_order, axis=0)
    cache_rows = ordered_cache.shape[1]
    all_slots = ordered_cache.shape[0]
    stored_key_rows = ordered_cache[:, :, 0].reshape(all_slots, cache_rows, heads_dev, head_dim)
    cache_values = ordered_cache[:, :, 1].reshape(all_slots, cache_rows, heads_dev, head_dim)
    all_lengths = jnp.take(window_lengths, request_order)
    positions = group_index * cache_rows + jnp.arange(cache_rows, dtype=jnp.int32)
    new_index = jnp.arange(token_count, dtype=jnp.int32)
    cache_limit = jnp.maximum(WIN - all_lengths[:, None], new_index[None, :] + 1)
    cache_mask = positions[None, None, None, :] >= cache_limit[:, :, None, None]

    sink_count = sink_cache.shape[2]
    anchor_key_rows = sink_cache[0][:, :, 0].reshape(slot_count, sink_count, heads_dev, head_dim)
    sink_values = sink_cache[0][:, :, 1].reshape(slot_count, sink_count, heads_dev, head_dim)
    qkv_matrix = w_qkv[0].reshape(width, 3 * local_width)
    conv_weights = conv_taps[0]
    scale = score_scale_table[0]
    gain_head = out_gain[0].reshape(heads_dev, head_dim)
    history = conv_history[0]
    fresh_mask = (new_index[None, :] <= new_index[:, None])[None, :, None, :]

    def layer(stream):
        normed = rms_scale(stream.astype(jnp.float32), pre_gain[0]).astype(jnp.bfloat16)
        projected = (
            jnp.dot(normed, qkv_matrix, preferred_element_type=jnp.float32)
            .astype(jnp.bfloat16)
            .reshape(slot_count, token_count, 3, local_width)
        )
        sequence = jnp.concatenate([history, projected], axis=1).astype(jnp.float32)
        taps = conv_weights.shape[0]
        mixed_rows = sum(
            sequence[:, i : i + token_count] * conv_weights[i][None, None] for i in range(taps)
        )
        activated = jax.nn.silu(mixed_rows)
        query_vec = unit_rows(activated[:, :, 0].reshape(slot_count, token_count, heads_dev, head_dim))
        key_vec = unit_rows(activated[:, :, 1].reshape(slot_count, token_count, heads_dev, head_dim))
        value_vec = activated[:, :, 2].reshape(slot_count, token_count, heads_dev, head_dim)
        beta_gate = jax.nn.sigmoid(
            jnp.dot(normed, w_beta[0], preferred_element_type=jnp.float32)
        ).reshape(slot_count, token_count, heads_dev)

        query_halfwidth = query_vec.astype(jnp.bfloat16)
        all_queries = spread(query_halfwidth, "req").reshape(
            all_slots, token_count, heads_dev, head_dim
        )
        stored_scores = (
            jnp.einsum(
                "rthd,rwhd->rthw",
                all_queries,
                stored_key_rows,
                preferred_element_type=jnp.float32,
            )
            * scale[None, None, :, None]
        )
        local_max = jnp.max(jnp.where(cache_mask, stored_scores, negative_big), axis=-1)
        local_weights = jnp.where(cache_mask, jnp.exp(stored_scores - local_max[..., None]), 0.0)
        local_sum = jnp.sum(local_weights, axis=-1)
        local_part = jnp.einsum(
            "rthw,rwhd->rthd",
            local_weights.astype(jnp.bfloat16),
            cache_values,
            preferred_element_type=jnp.float32,
        )
        stats = jnp.concatenate(
            [
                local_sum,
                local_max,
                jnp.zeros((all_slots, token_count, head_dim - 2 * heads_dev), jnp.float32),
            ],
            axis=-1,
        )
        packed = jnp.concatenate([local_part, stats[:, :, None, :]], axis=2).reshape(
            groups, slot_count, token_count, heads_dev + 1, head_dim
        )
        gathered = lax.all_to_all(packed, "req", 0, 0, tiled=True)
        part_numer = gathered[:, :, :, :heads_dev]
        part_sum = gathered[:, :, :, heads_dev, :heads_dev]
        part_max = gathered[:, :, :, heads_dev, heads_dev : 2 * heads_dev]

        delta_state, readout = delta_rule(start_state, key_vec, query_vec, value_vec, beta_gate)

        new_keys = key_vec.astype(jnp.bfloat16)
        new_values = value_vec.astype(jnp.bfloat16)
        anchor_scores = (
            jnp.einsum(
                "sthd,sjhd->sthj", query_halfwidth, anchor_key_rows, preferred_element_type=jnp.float32
            )
            * scale[None, None, :, None]
        )
        incoming_scores = (
            jnp.einsum(
                "sthd,suhd->sthu", query_halfwidth, new_keys, preferred_element_type=jnp.float32
            )
            * scale[None, None, :, None]
        )
        highest = jnp.maximum(
            jnp.max(anchor_scores, axis=-1),
            jnp.max(jnp.where(fresh_mask, incoming_scores, negative_big), axis=-1),
        )
        highest = jnp.maximum(highest, jnp.max(part_max, axis=0))
        part_scale = jnp.exp(part_max - highest[None])
        sink_weights = jnp.exp(anchor_scores - highest[..., None])
        fresh_weights = jnp.where(fresh_mask, jnp.exp(incoming_scores - highest[..., None]), 0.0)
        weight_sum = (
            jnp.sum(part_scale * part_sum, axis=0)
            + jnp.sum(sink_weights, axis=-1)
            + jnp.sum(fresh_weights, axis=-1)
        )
        numerator = jnp.sum(part_scale[..., None] * part_numer, axis=0)
        numerator = numerator + jnp.einsum(
            "sthj,sjhd->sthd",
            sink_weights.astype(jnp.bfloat16),
            sink_values,
            preferred_element_type=jnp.float32,
        )
        numerator = numerator + jnp.einsum(
            "sthu,suhd->sthd",
            fresh_weights.astype(jnp.bfloat16),
            new_values,
            preferred_element_type=jnp.float32,
        )
        attended = numerator / weight_sum[..., None]
        mixed_heads = (
            (rms_scale(readout, gain_head[None, None]) + attended)
            .astype(jnp.bfloat16)
            .reshape(rows, local_width)
        )
        partial_out = jnp.dot(mixed_heads, w_out[0], preferred_element_type=jnp.float32)
        mixer_out = head_sum(partial_out)
        stream_out = (stream.astype(jnp.float32) + mixer_out).astype(jnp.bfloat16)
        return stream_out, delta_state

    first_out, first_state = layer(embedded)
    received = lax.ppermute(first_out, "section", [(0, 1)])
    second_out, second_state = layer(received)
    is_first = section_index == 0
    produced = jnp.where(is_first, first_out, second_out).reshape(slot_count, token_count, width)
    final_state = jnp.where(is_first, first_state, second_state)
    return (produced[None], final_state[None])


def solution(mesh):
    return jax.shard_map(
        shards,
        mesh=mesh,
        in_specs=(
            P("req", None),
            P(),
            P(),
            P(("req", "head"), None),
            P("section", None, "req", None, "head"),
            P("section", None, "req", "head", None),
            P("section", "req", None, None, "head"),
            P("section", "req", None, None, "head"),
            P("section", None, None, "head"),
            P("section", "head", None),
            P("section", None, "head"),
            P("section", None, None, "head"),
            P("section", None),
            P("section", "head"),
            P("section", "head"),
        ),
        out_specs=(P("section", "req", None, None), P("section", "req", None, "head", None)),
        check_vma=False,
    )
```

```python
import jax
import jax.numpy as jnp
from jax import lax
from jax.experimental import pallas as pl
from jax.experimental.pallas import tpu as pltpu
from jax.sharding import PartitionSpec as P

WIN = 512


epsilon = 1e-06
negative_big = -1e30


def rms_scale(values, gain_row):
    return (
        values * lax.rsqrt(jnp.mean(values * values, axis=-1, keepdims=True) + epsilon) * gain_row
    )


def unit_rows(values):
    return values * lax.rsqrt(jnp.sum(values * values, axis=-1, keepdims=True) + epsilon)


def spread(value, axis):
    peers = lax.axis_size(axis)
    copies = jnp.broadcast_to(value[None], (peers,) + value.shape)
    return lax.all_to_all(copies, axis, 0, 0, tiled=True)


def head_sum(value):
    peers = lax.axis_size("head")
    step = 1
    while step < peers:
        pairs = [(i, i ^ step) for i in range(peers)]
        value = value + lax.ppermute(value, "head", pairs)
        step *= 2
    return value


def delta_rule_kernel(beta_ref, state_ref, key_ref, query_ref, value_ref, state_out, read_out):
    slots, key_rows, _ = state_ref.shape
    heads = key_ref.shape[1]
    tokens = value_ref.shape[1]
    def one_block(index, carry):
        s = index // heads
        h = index % heads
        cols = pl.ds(pl.multiple_of(h * key_rows, key_rows), key_rows)
        matrix = state_ref[s, :, cols]
        key_cols = key_ref[s, h]
        query_cols = query_ref[s, h]
        for t in range(tokens):
            k_t = key_cols[:, t : t + 1]
            predicted = jnp.sum(matrix * k_t, axis=0, keepdims=True)
            v_t = value_ref[s, pl.ds(t, 1), cols]
            gate = beta_ref[(s * tokens + t) * heads + h]
            matrix = matrix + gate * (k_t * (v_t - predicted))
            read_out[s, pl.ds(t, 1), cols] = jnp.sum(
                matrix * query_cols[:, t : t + 1], axis=0, keepdims=True
            )
        state_out[s, :, cols] = matrix
        return carry

    lax.fori_loop(0, slots * heads, one_block, 0)


def delta_rule(start_state, key_vec, query_vec, value_vec, beta_gate):
    slots, key_rows, heads, value_cols = start_state.shape
    tokens = key_vec.shape[1]
    vmem = pl.BlockSpec(memory_space=pltpu.VMEM)
    new_state, readout = pl.pallas_call(
        delta_rule_kernel,
        out_shape=(
            jax.ShapeDtypeStruct((slots, key_rows, heads * value_cols), jnp.float32),
            jax.ShapeDtypeStruct((slots, tokens, heads * value_cols), jnp.float32),
        ),
        in_specs=[pl.BlockSpec(memory_space=pltpu.SMEM), vmem, vmem, vmem, vmem],
        out_specs=(vmem, vmem),
        cost_estimate=pl.CostEstimate(
            flops=8 * slots * heads * tokens * key_rows * value_cols,
            bytes_accessed=8 * slots * key_rows * heads * value_cols,
            transcendentals=0,
        ),
    )(
        beta_gate.reshape(-1),
        start_state.reshape(slots, key_rows, heads * value_cols),
        jnp.transpose(key_vec, (0, 2, 3, 1)),
        jnp.transpose(query_vec, (0, 2, 3, 1)),
        value_vec.reshape(slots, tokens, heads * value_cols),
    )
    return (
        new_state.reshape(slots, key_rows, heads, value_cols),
        readout.reshape(slots, tokens, heads, value_cols),
    )


def shards(
    token_ids,
    request_order,
    window_lengths,
    embed_table,
    cache_arrived,
    state_arrived,
    conv_history,
    sink_cache,
    w_qkv,
    w_out,
    w_beta,
    conv_taps,
    pre_gain,
    out_gain,
    score_scale_table,
):
    slot_count, token_count = token_ids.shape
    groups = lax.axis_size("req")
    heads_dev = score_scale_table.shape[1]
    width = pre_gain.shape[1]
    local_width = out_gain.shape[1]
    head_dim = local_width // heads_dev
    group_index = lax.axis_index("req")
    section_index = lax.axis_index("section")
    vocab_dev = embed_table.shape[0]
    rows = slot_count * token_count

    all_ids = spread(token_ids, "req")
    first_row = lax.axis_index(("req", "head")) * vocab_dev
    onehot = (
        all_ids.reshape(-1)[:, None] == first_row + jnp.arange(vocab_dev, dtype=jnp.int32)[None, :]
    ).astype(jnp.bfloat16)
    looked_up = jnp.dot(onehot, embed_table, preferred_element_type=jnp.float32).astype(jnp.bfloat16)
    arrived_rows = lax.all_to_all(
        looked_up.reshape(groups, rows, width), "req", 0, 0, tiled=True
    )
    partial_rows = jnp.sum(arrived_rows.astype(jnp.float32), axis=0).astype(jnp.bfloat16)
    embedded = jnp.sum(spread(partial_rows, "head").astype(jnp.float32), axis=0).astype(jnp.bfloat16)

    ordered_states = jnp.take(state_arrived[0], request_order, axis=0)
    start_state = lax.all_to_all(ordered_states, "req", 0, 1, tiled=True)

    all_slots, cache_rows = cache_arrived.shape[1], cache_arrived.shape[2]
    by_head = jnp.transpose(
        cache_arrived[0].reshape(all_slots, cache_rows, 2, heads_dev, head_dim), (2, 0, 3, 1, 4)
    )
    ordered_cache = jnp.take(by_head, request_order, axis=1)
    stored_key_rows = ordered_cache[0]
    cache_values = ordered_cache[1]
    all_lengths = jnp.take(window_lengths, request_order)
    positions = group_index * cache_rows + jnp.arange(cache_rows, dtype=jnp.int32)
    new_index = jnp.arange(token_count, dtype=jnp.int32)
    cache_limit = jnp.maximum(WIN - all_lengths[:, None], new_index[None, :] + 1)
    cache_mask = positions[None, None, None, :] >= cache_limit[:, :, None, None]

    sink_count = sink_cache.shape[2]
    anchor_key_rows = sink_cache[0][:, :, 0].reshape(slot_count, sink_count, heads_dev, head_dim)
    sink_values = sink_cache[0][:, :, 1].reshape(slot_count, sink_count, heads_dev, head_dim)
    qkv_matrix = w_qkv[0].reshape(width, 3 * local_width)
    conv_weights = conv_taps[0]
    scale = score_scale_table[0]
    gain_head = out_gain[0].reshape(heads_dev, head_dim)
    history = conv_history[0]
    fresh_mask = (new_index[None, :] <= new_index[:, None])[None, :, None, :]

    def layer(stream):
        normed = rms_scale(stream.astype(jnp.float32), pre_gain[0]).astype(jnp.bfloat16)
        projected = (
            jnp.dot(normed, qkv_matrix, preferred_element_type=jnp.float32)
            .astype(jnp.bfloat16)
            .reshape(slot_count, token_count, 3, local_width)
        )
        sequence = jnp.concatenate([history, projected], axis=1).astype(jnp.float32)
        taps = conv_weights.shape[0]
        mixed_rows = sum(
            sequence[:, i : i + token_count] * conv_weights[i][None, None] for i in range(taps)
        )
        activated = jax.nn.silu(mixed_rows)
        query_vec = unit_rows(activated[:, :, 0].reshape(slot_count, token_count, heads_dev, head_dim))
        key_vec = unit_rows(activated[:, :, 1].reshape(slot_count, token_count, heads_dev, head_dim))
        value_vec = activated[:, :, 2].reshape(slot_count, token_count, heads_dev, head_dim)
        beta_gate = jax.nn.sigmoid(
            jnp.dot(normed, w_beta[0], preferred_element_type=jnp.float32)
        ).reshape(slot_count, token_count, heads_dev)

        query_halfwidth = query_vec.astype(jnp.bfloat16)
        all_queries = spread(query_halfwidth, "req").reshape(
            all_slots, token_count, heads_dev, head_dim
        )
        stored_scores = (
            jnp.einsum(
                "rthd,rhwd->rthw",
                all_queries,
                stored_key_rows,
                preferred_element_type=jnp.float32,
            )
            * scale[None, None, :, None]
        )
        local_max = jnp.max(jnp.where(cache_mask, stored_scores, negative_big), axis=-1)
        local_weights = jnp.where(cache_mask, jnp.exp(stored_scores - local_max[..., None]), 0.0)
        local_sum = jnp.sum(local_weights, axis=-1)
        local_part = jnp.einsum(
            "rthw,rhwd->rthd",
            local_weights.astype(jnp.bfloat16),
            cache_values,
            preferred_element_type=jnp.float32,
        )
        stats = jnp.concatenate(
            [
                local_sum,
                local_max,
                jnp.zeros((all_slots, token_count, head_dim - 2 * heads_dev), jnp.float32),
            ],
            axis=-1,
        )
        packed = jnp.concatenate([local_part, stats[:, :, None, :]], axis=2).reshape(
            groups, slot_count, token_count, heads_dev + 1, head_dim
        )
        gathered = lax.all_to_all(packed, "req", 0, 0, tiled=True)
        part_numer = gathered[:, :, :, :heads_dev]
        part_sum = gathered[:, :, :, heads_dev, :heads_dev]
        part_max = gathered[:, :, :, heads_dev, heads_dev : 2 * heads_dev]

        delta_state, readout = delta_rule(start_state, key_vec, query_vec, value_vec, beta_gate)

        new_keys = key_vec.astype(jnp.bfloat16)
        new_values = value_vec.astype(jnp.bfloat16)
        anchor_scores = (
            jnp.einsum(
                "sthd,sjhd->sthj", query_halfwidth, anchor_key_rows, preferred_element_type=jnp.float32
            )
            * scale[None, None, :, None]
        )
        incoming_scores = (
            jnp.einsum(
                "sthd,suhd->sthu", query_halfwidth, new_keys, preferred_element_type=jnp.float32
            )
            * scale[None, None, :, None]
        )
        highest = jnp.maximum(
            jnp.max(anchor_scores, axis=-1),
            jnp.max(jnp.where(fresh_mask, incoming_scores, negative_big), axis=-1),
        )
        highest = jnp.maximum(highest, jnp.max(part_max, axis=0))
        part_scale = jnp.exp(part_max - highest[None])
        sink_weights = jnp.exp(anchor_scores - highest[..., None])
        fresh_weights = jnp.where(fresh_mask, jnp.exp(incoming_scores - highest[..., None]), 0.0)
        weight_sum = (
            jnp.sum(part_scale * part_sum, axis=0)
            + jnp.sum(sink_weights, axis=-1)
            + jnp.sum(fresh_weights, axis=-1)
        )
        numerator = jnp.sum(part_scale[..., None] * part_numer, axis=0)
        numerator = numerator + jnp.einsum(
            "sthj,sjhd->sthd",
            sink_weights.astype(jnp.bfloat16),
            sink_values,
            preferred_element_type=jnp.float32,
        )
        numerator = numerator + jnp.einsum(
            "sthu,suhd->sthd",
            fresh_weights.astype(jnp.bfloat16),
            new_values,
            preferred_element_type=jnp.float32,
        )
        attended = numerator / weight_sum[..., None]
        mixed_heads = (
            (rms_scale(readout, gain_head[None, None]) + attended)
            .astype(jnp.bfloat16)
            .reshape(rows, local_width)
        )
        partial_out = jnp.dot(mixed_heads, w_out[0], preferred_element_type=jnp.float32)
        mixer_out = head_sum(partial_out)
        stream_out = (stream.astype(jnp.float32) + mixer_out).astype(jnp.bfloat16)
        return stream_out, delta_state

    first_out, first_state = layer(embedded)
    received = lax.ppermute(first_out, "section", [(0, 1)])
    second_out, second_state = layer(received)
    is_first = section_index == 0
    produced = jnp.where(is_first, first_out, second_out).reshape(slot_count, token_count, width)
    final_state = jnp.where(is_first, first_state, second_state)
    return (produced[None], final_state[None])


def solution(mesh):
    return jax.shard_map(
        shards,
        mesh=mesh,
        in_specs=(
            P("req", None),
            P(),
            P(),
            P(("req", "head"), None),
            P("section", None, "req", None, "head"),
            P("section", None, "req", "head", None),
            P("section", "req", None, None, "head"),
            P("section", "req", None, None, "head"),
            P("section", None, None, "head"),
            P("section", "head", None),
            P("section", None, "head"),
            P("section", None, None, "head"),
            P("section", None),
            P("section", "head"),
            P("section", "head"),
        ),
        out_specs=(P("section", "req", None, None), P("section", "req", None, "head", None)),
        check_vma=False,
    )
```

```python
import jax
import jax.numpy as jnp
from jax import lax
from jax.experimental import pallas as pl
from jax.experimental.pallas import tpu as pltpu
from jax.sharding import PartitionSpec as P

WIN = 512


epsilon = 1e-06
negative_big = -1e30


def rms_scale(values, gain_row):
    return (
        values * lax.rsqrt(jnp.mean(values * values, axis=-1, keepdims=True) + epsilon) * gain_row
    )


def unit_rows(values):
    return values * lax.rsqrt(jnp.sum(values * values, axis=-1, keepdims=True) + epsilon)


def spread(value, axis):
    peers = lax.axis_size(axis)
    copies = jnp.broadcast_to(value[None], (peers,) + value.shape)
    return lax.all_to_all(copies, axis, 0, 0, tiled=True)


def head_sum(value):
    peers = lax.axis_size("head")
    step = 1
    while step < peers:
        pairs = [(i, i ^ step) for i in range(peers)]
        value = value + lax.ppermute(value, "head", pairs)
        step *= 2
    return value


def delta_rule_kernel(beta_ref, state_ref, key_ref, query_ref, value_ref, state_out, read_out):
    slots, key_rows, _ = state_ref.shape
    heads = key_ref.shape[1]
    tokens = value_ref.shape[1]
    def one_block(index, carry):
        s = index // heads
        h = index % heads
        cols = pl.ds(pl.multiple_of(h * key_rows, key_rows), key_rows)
        matrix = state_ref[s, :, cols]
        key_cols = key_ref[s, h]
        query_cols = query_ref[s, h]
        for t in range(tokens):
            k_t = key_cols[:, t : t + 1]
            predicted = jnp.sum(matrix * k_t, axis=0, keepdims=True)
            v_t = value_ref[s, pl.ds(t, 1), cols]
            gate = beta_ref[(s * tokens + t) * heads + h]
            matrix = matrix + gate * (k_t * (v_t - predicted))
            read_out[s, pl.ds(t, 1), cols] = jnp.sum(
                matrix * query_cols[:, t : t + 1], axis=0, keepdims=True
            )
        state_out[s, :, cols] = matrix
        return carry

    lax.fori_loop(0, slots * heads, one_block, 0)


def delta_rule(start_state, key_vec, query_vec, value_vec, beta_gate):
    slots, key_rows, heads, value_cols = start_state.shape
    tokens = key_vec.shape[1]
    vmem = pl.BlockSpec(memory_space=pltpu.VMEM)
    new_state, readout = pl.pallas_call(
        delta_rule_kernel,
        out_shape=(
            jax.ShapeDtypeStruct((slots, key_rows, heads * value_cols), jnp.float32),
            jax.ShapeDtypeStruct((slots, tokens, heads * value_cols), jnp.float32),
        ),
        in_specs=[pl.BlockSpec(memory_space=pltpu.SMEM), vmem, vmem, vmem, vmem],
        out_specs=(vmem, vmem),
        cost_estimate=pl.CostEstimate(
            flops=8 * slots * heads * tokens * key_rows * value_cols,
            bytes_accessed=8 * slots * key_rows * heads * value_cols,
            transcendentals=0,
        ),
    )(
        beta_gate.reshape(-1),
        start_state.reshape(slots, key_rows, heads * value_cols),
        jnp.transpose(key_vec, (0, 2, 3, 1)),
        jnp.transpose(query_vec, (0, 2, 3, 1)),
        value_vec.reshape(slots, tokens, heads * value_cols),
    )
    return (
        new_state.reshape(slots, key_rows, heads, value_cols),
        readout.reshape(slots, tokens, heads, value_cols),
    )


def shards(
    token_ids,
    request_order,
    window_lengths,
    embed_table,
    cache_arrived,
    state_arrived,
    conv_history,
    sink_cache,
    w_qkv,
    w_out,
    w_beta,
    conv_taps,
    pre_gain,
    out_gain,
    score_scale_table,
):
    slot_count, token_count = token_ids.shape
    groups = lax.axis_size("req")
    heads_dev = score_scale_table.shape[1]
    width = pre_gain.shape[1]
    local_width = out_gain.shape[1]
    head_dim = local_width // heads_dev
    group_index = lax.axis_index("req")
    section_index = lax.axis_index("section")
    vocab_dev = embed_table.shape[0]
    rows = slot_count * token_count

    all_ids = spread(token_ids, "req")
    first_row = lax.axis_index(("req", "head")) * vocab_dev
    onehot = (
        all_ids.reshape(-1)[:, None] == first_row + jnp.arange(vocab_dev, dtype=jnp.int32)[None, :]
    ).astype(jnp.bfloat16)
    looked_up = jnp.dot(onehot, embed_table, preferred_element_type=jnp.float32).astype(jnp.bfloat16)
    arrived_rows = lax.all_to_all(
        looked_up.reshape(groups, rows, width), "req", 0, 0, tiled=True
    )
    partial_rows = jnp.sum(arrived_rows.astype(jnp.float32), axis=0).astype(jnp.bfloat16)
    embedded = jnp.sum(spread(partial_rows, "head").astype(jnp.float32), axis=0).astype(jnp.bfloat16)

    ordered_states = jnp.take(state_arrived[0], request_order, axis=0)
    start_state = lax.all_to_all(ordered_states, "req", 0, 1, tiled=True)

    all_slots, cache_rows = cache_arrived.shape[1], cache_arrived.shape[2]
    by_head = jnp.transpose(
        cache_arrived[0].reshape(all_slots, cache_rows, 2, heads_dev, head_dim), (2, 0, 3, 1, 4)
    )
    ordered_cache = jnp.take(by_head, request_order, axis=1)
    stored_key_rows = ordered_cache[0]
    cache_values = ordered_cache[1]
    all_lengths = jnp.take(window_lengths, request_order)
    positions = group_index * cache_rows + jnp.arange(cache_rows, dtype=jnp.int32)
    new_index = jnp.arange(token_count, dtype=jnp.int32)
    cache_limit = jnp.maximum(WIN - all_lengths[:, None], new_index[None, :] + 1)
    cache_mask = positions[None, None, None, :] >= cache_limit[:, :, None, None]

    sink_count = sink_cache.shape[2]
    anchor_key_rows = sink_cache[0][:, :, 0].reshape(slot_count, sink_count, heads_dev, head_dim)
    sink_values = sink_cache[0][:, :, 1].reshape(slot_count, sink_count, heads_dev, head_dim)
    qkv_matrix = w_qkv[0].reshape(width, 3 * local_width)
    conv_weights = conv_taps[0]
    scale = score_scale_table[0]
    gain_head = out_gain[0].reshape(heads_dev, head_dim)
    history = conv_history[0]
    home_mask = jnp.concatenate(
        [
            jnp.ones((token_count, sink_count), jnp.bool_),
            new_index[None, :] <= new_index[:, None],
        ],
        axis=1,
    )[None, :, None, :]

    def layer(stream):
        normed = rms_scale(stream.astype(jnp.float32), pre_gain[0]).astype(jnp.bfloat16)
        projected = (
            jnp.dot(normed, qkv_matrix, preferred_element_type=jnp.float32)
            .astype(jnp.bfloat16)
            .reshape(slot_count, token_count, 3, local_width)
        )
        sequence = jnp.concatenate([history, projected], axis=1).astype(jnp.float32)
        taps = conv_weights.shape[0]
        mixed_rows = sum(
            sequence[:, i : i + token_count] * conv_weights[i][None, None] for i in range(taps)
        )
        activated = jax.nn.silu(mixed_rows)
        query_vec = unit_rows(activated[:, :, 0].reshape(slot_count, token_count, heads_dev, head_dim))
        key_vec = unit_rows(activated[:, :, 1].reshape(slot_count, token_count, heads_dev, head_dim))
        value_vec = activated[:, :, 2].reshape(slot_count, token_count, heads_dev, head_dim)
        beta_gate = jax.nn.sigmoid(
            jnp.dot(normed, w_beta[0], preferred_element_type=jnp.float32)
        ).reshape(slot_count, token_count, heads_dev)

        query_halfwidth = query_vec.astype(jnp.bfloat16)
        all_queries = spread(query_halfwidth, "req").reshape(
            all_slots, token_count, heads_dev, head_dim
        )
        stored_scores = (
            jnp.einsum(
                "rthd,rhwd->rthw",
                all_queries,
                stored_key_rows,
                preferred_element_type=jnp.float32,
            )
            * scale[None, None, :, None]
        )
        local_max = jnp.max(jnp.where(cache_mask, stored_scores, negative_big), axis=-1)
        local_weights = jnp.where(cache_mask, jnp.exp(stored_scores - local_max[..., None]), 0.0)
        local_sum = jnp.sum(local_weights, axis=-1)
        local_part = jnp.einsum(
            "rthw,rhwd->rthd",
            local_weights.astype(jnp.bfloat16),
            cache_values,
            preferred_element_type=jnp.float32,
        )
        stats = jnp.concatenate(
            [
                local_sum,
                local_max,
                jnp.zeros((all_slots, token_count, head_dim - 2 * heads_dev), jnp.float32),
            ],
            axis=-1,
        )
        packed = jnp.concatenate([local_part, stats[:, :, None, :]], axis=2).reshape(
            groups, slot_count, token_count, heads_dev + 1, head_dim
        )
        gathered = lax.all_to_all(packed, "req", 0, 0, tiled=True)
        part_numer = gathered[:, :, :, :heads_dev]
        part_sum = gathered[:, :, :, heads_dev, :heads_dev]
        part_max = gathered[:, :, :, heads_dev, heads_dev : 2 * heads_dev]

        delta_state, readout = delta_rule(start_state, key_vec, query_vec, value_vec, beta_gate)

        home_keys = jnp.concatenate([anchor_key_rows, key_vec.astype(jnp.bfloat16)], axis=1)
        home_values = jnp.concatenate([sink_values, value_vec.astype(jnp.bfloat16)], axis=1)
        home_scores = (
            jnp.einsum(
                "sthd,sjhd->sthj", query_halfwidth, home_keys, preferred_element_type=jnp.float32
            )
            * scale[None, None, :, None]
        )
        home_max = jnp.max(jnp.where(home_mask, home_scores, negative_big), axis=-1)
        home_weights = jnp.where(home_mask, jnp.exp(home_scores - home_max[..., None]), 0.0)
        home_sum = jnp.sum(home_weights, axis=-1)
        home_part = jnp.einsum(
            "sthj,sjhd->sthd",
            home_weights.astype(jnp.bfloat16),
            home_values,
            preferred_element_type=jnp.float32,
        )
        highest = jnp.maximum(home_max, jnp.max(part_max, axis=0))
        part_scale = jnp.exp(part_max - highest[None])
        home_scale = jnp.exp(home_max - highest)
        weight_sum = home_scale * home_sum + jnp.sum(part_scale * part_sum, axis=0)
        numerator = home_scale[..., None] * home_part + jnp.sum(
            part_scale[..., None] * part_numer, axis=0
        )
        attended = numerator / weight_sum[..., None]
        mixed_heads = (
            (rms_scale(readout, gain_head[None, None]) + attended)
            .astype(jnp.bfloat16)
            .reshape(rows, local_width)
        )
        partial_out = jnp.dot(mixed_heads, w_out[0], preferred_element_type=jnp.float32)
        mixer_out = head_sum(partial_out)
        stream_out = (stream.astype(jnp.float32) + mixer_out).astype(jnp.bfloat16)
        return stream_out, delta_state

    first_out, first_state = layer(embedded)
    received = lax.ppermute(first_out, "section", [(0, 1)])
    second_out, second_state = layer(received)
    is_first = section_index == 0
    produced = jnp.where(is_first, first_out, second_out).reshape(slot_count, token_count, width)
    final_state = jnp.where(is_first, first_state, second_state)
    return (produced[None], final_state[None])


def solution(mesh):
    return jax.shard_map(
        shards,
        mesh=mesh,
        in_specs=(
            P("req", None),
            P(),
            P(),
            P(("req", "head"), None),
            P("section", None, "req", None, "head"),
            P("section", None, "req", "head", None),
            P("section", "req", None, None, "head"),
            P("section", "req", None, None, "head"),
            P("section", None, None, "head"),
            P("section", "head", None),
            P("section", None, "head"),
            P("section", None, None, "head"),
            P("section", None),
            P("section", "head"),
            P("section", "head"),
        ),
        out_specs=(P("section", "req", None, None), P("section", "req", None, "head", None)),
        check_vma=False,
    )
```

```python
import jax
import jax.numpy as jnp
from jax import lax
from jax.experimental import pallas as pl
from jax.experimental.pallas import tpu as pltpu
from jax.sharding import PartitionSpec as P

WIN = 512


epsilon = 1e-06
negative_big = -1e30


def rms_scale(values, gain_row):
    return (
        values * lax.rsqrt(jnp.mean(values * values, axis=-1, keepdims=True) + epsilon) * gain_row
    )


def unit_rows(values):
    return values * lax.rsqrt(jnp.sum(values * values, axis=-1, keepdims=True) + epsilon)


def spread(value, axis):
    peers = lax.axis_size(axis)
    copies = jnp.broadcast_to(value[None], (peers,) + value.shape)
    return lax.all_to_all(copies, axis, 0, 0, tiled=True)


def head_sum(value):
    peers = lax.axis_size("head")
    step = 1
    while step < peers:
        pairs = [(i, i ^ step) for i in range(peers)]
        value = value + lax.ppermute(value, "head", pairs)
        step *= 2
    return value


def delta_rule_kernel(beta_ref, state_ref, key_ref, query_ref, value_ref, state_out, read_out):
    slots, key_rows, _ = state_ref.shape
    heads = key_ref.shape[1]
    tokens = value_ref.shape[1]
    def one_block(index, carry):
        s = index // heads
        h = index % heads
        cols = pl.ds(pl.multiple_of(h * key_rows, key_rows), key_rows)
        matrix = state_ref[s, :, cols]
        key_cols = key_ref[s, h]
        query_cols = query_ref[s, h]
        for t in range(tokens):
            k_t = key_cols[:, t : t + 1]
            predicted = jnp.sum(matrix * k_t, axis=0, keepdims=True)
            v_t = value_ref[s, pl.ds(t, 1), cols]
            gate = beta_ref[(s * tokens + t) * heads + h]
            matrix = matrix + gate * (k_t * (v_t - predicted))
            read_out[s, pl.ds(t, 1), cols] = jnp.sum(
                matrix * query_cols[:, t : t + 1], axis=0, keepdims=True
            )
        state_out[s, :, cols] = matrix
        return carry

    lax.fori_loop(0, slots * heads, one_block, 0)


def delta_rule(start_state, key_vec, query_vec, value_vec, beta_gate):
    slots, key_rows, heads, value_cols = start_state.shape
    tokens = key_vec.shape[1]
    vmem = pl.BlockSpec(memory_space=pltpu.VMEM)
    new_state, readout = pl.pallas_call(
        delta_rule_kernel,
        out_shape=(
            jax.ShapeDtypeStruct((slots, key_rows, heads * value_cols), jnp.float32),
            jax.ShapeDtypeStruct((slots, tokens, heads * value_cols), jnp.float32),
        ),
        in_specs=[pl.BlockSpec(memory_space=pltpu.SMEM), vmem, vmem, vmem, vmem],
        out_specs=(vmem, vmem),
        cost_estimate=pl.CostEstimate(
            flops=8 * slots * heads * tokens * key_rows * value_cols,
            bytes_accessed=8 * slots * key_rows * heads * value_cols,
            transcendentals=0,
        ),
    )(
        beta_gate.reshape(-1),
        start_state.reshape(slots, key_rows, heads * value_cols),
        jnp.transpose(key_vec, (0, 2, 3, 1)),
        jnp.transpose(query_vec, (0, 2, 3, 1)),
        value_vec.reshape(slots, tokens, heads * value_cols),
    )
    return (
        new_state.reshape(slots, key_rows, heads, value_cols),
        readout.reshape(slots, tokens, heads, value_cols),
    )


def shards(
    token_ids,
    request_order,
    window_lengths,
    embed_table,
    cache_arrived,
    state_arrived,
    conv_history,
    sink_cache,
    w_qkv,
    w_out,
    w_beta,
    conv_taps,
    pre_gain,
    out_gain,
    score_scale_table,
):
    slot_count, token_count = token_ids.shape
    groups = lax.axis_size("req")
    heads_dev = score_scale_table.shape[1]
    width = pre_gain.shape[1]
    local_width = out_gain.shape[1]
    head_dim = local_width // heads_dev
    group_index = lax.axis_index("req")
    section_index = lax.axis_index("section")
    vocab_dev = embed_table.shape[0]
    rows = slot_count * token_count

    half = token_count // 2
    all_ids = lax.dynamic_slice_in_dim(spread(token_ids, "req"), section_index * half, half, 2)
    first_row = lax.axis_index(("req", "head")) * vocab_dev
    onehot = (
        all_ids.reshape(-1)[:, None] == first_row + jnp.arange(vocab_dev, dtype=jnp.int32)[None, :]
    ).astype(jnp.bfloat16)
    looked_up = jnp.dot(onehot, embed_table, preferred_element_type=jnp.float32).astype(jnp.bfloat16)
    arrived_rows = lax.all_to_all(
        looked_up.reshape(groups, slot_count * half, width), "req", 0, 0, tiled=True
    )
    partial_rows = jnp.sum(arrived_rows.astype(jnp.float32), axis=0).astype(jnp.bfloat16)
    own_half = (
        jnp.sum(spread(partial_rows, "head").astype(jnp.float32), axis=0)
        .astype(jnp.bfloat16)
        .reshape(slot_count, half, width)
    )
    other_half = lax.ppermute(own_half, "section", [(0, 1), (1, 0)])
    embedded = jnp.concatenate([own_half, other_half], axis=1).reshape(rows, width)

    ordered_states = jnp.take(state_arrived[0], request_order, axis=0)
    start_state = lax.all_to_all(ordered_states, "req", 0, 1, tiled=True)

    all_slots, cache_rows = cache_arrived.shape[1], cache_arrived.shape[2]
    by_head = jnp.transpose(
        cache_arrived[0].reshape(all_slots, cache_rows, 2, heads_dev, head_dim), (2, 0, 3, 1, 4)
    )
    ordered_cache = jnp.take(by_head, request_order, axis=1)
    stored_key_rows = ordered_cache[0]
    cache_values = ordered_cache[1]
    all_lengths = jnp.take(window_lengths, request_order)
    positions = group_index * cache_rows + jnp.arange(cache_rows, dtype=jnp.int32)
    new_index = jnp.arange(token_count, dtype=jnp.int32)
    cache_limit = jnp.maximum(WIN - all_lengths[:, None], new_index[None, :] + 1)
    cache_mask = positions[None, None, None, :] >= cache_limit[:, :, None, None]

    sink_count = sink_cache.shape[2]
    anchor_key_rows = sink_cache[0][:, :, 0].reshape(slot_count, sink_count, heads_dev, head_dim)
    sink_values = sink_cache[0][:, :, 1].reshape(slot_count, sink_count, heads_dev, head_dim)
    qkv_matrix = w_qkv[0].reshape(width, 3 * local_width)
    conv_weights = conv_taps[0]
    scale = score_scale_table[0]
    gain_head = out_gain[0].reshape(heads_dev, head_dim)
    history = conv_history[0]
    home_mask = jnp.concatenate(
        [
            jnp.ones((token_count, sink_count), jnp.bool_),
            new_index[None, :] <= new_index[:, None],
        ],
        axis=1,
    )[None, :, None, :]

    def layer(stream):
        normed = rms_scale(stream.astype(jnp.float32), pre_gain[0]).astype(jnp.bfloat16)
        projected = (
            jnp.dot(normed, qkv_matrix, preferred_element_type=jnp.float32)
            .astype(jnp.bfloat16)
            .reshape(slot_count, token_count, 3, local_width)
        )
        sequence = jnp.concatenate([history, projected], axis=1).astype(jnp.float32)
        taps = conv_weights.shape[0]
        mixed_rows = sum(
            sequence[:, i : i + token_count] * conv_weights[i][None, None] for i in range(taps)
        )
        activated = jax.nn.silu(mixed_rows)
        query_vec = unit_rows(activated[:, :, 0].reshape(slot_count, token_count, heads_dev, head_dim))
        key_vec = unit_rows(activated[:, :, 1].reshape(slot_count, token_count, heads_dev, head_dim))
        value_vec = activated[:, :, 2].reshape(slot_count, token_count, heads_dev, head_dim)
        beta_gate = jax.nn.sigmoid(
            jnp.dot(normed, w_beta[0], preferred_element_type=jnp.float32)
        ).reshape(slot_count, token_count, heads_dev)

        query_halfwidth = query_vec.astype(jnp.bfloat16)
        all_queries = spread(query_halfwidth, "req").reshape(
            all_slots, token_count, heads_dev, head_dim
        )
        stored_scores = (
            jnp.einsum(
                "rthd,rhwd->rthw",
                all_queries,
                stored_key_rows,
                preferred_element_type=jnp.float32,
            )
            * scale[None, None, :, None]
        )
        local_max = jnp.max(jnp.where(cache_mask, stored_scores, negative_big), axis=-1)
        local_weights = jnp.where(cache_mask, jnp.exp(stored_scores - local_max[..., None]), 0.0)
        local_sum = jnp.sum(local_weights, axis=-1)
        local_part = jnp.einsum(
            "rthw,rhwd->rthd",
            local_weights.astype(jnp.bfloat16),
            cache_values,
            preferred_element_type=jnp.float32,
        )
        stats = jnp.concatenate(
            [
                local_sum,
                local_max,
                jnp.zeros((all_slots, token_count, head_dim - 2 * heads_dev), jnp.float32),
            ],
            axis=-1,
        )
        packed = jnp.concatenate([local_part, stats[:, :, None, :]], axis=2).reshape(
            groups, slot_count, token_count, heads_dev + 1, head_dim
        )
        gathered = lax.all_to_all(packed, "req", 0, 0, tiled=True)
        part_numer = gathered[:, :, :, :heads_dev]
        part_sum = gathered[:, :, :, heads_dev, :heads_dev]
        part_max = gathered[:, :, :, heads_dev, heads_dev : 2 * heads_dev]

        delta_state, readout = delta_rule(start_state, key_vec, query_vec, value_vec, beta_gate)

        home_keys = jnp.concatenate([anchor_key_rows, key_vec.astype(jnp.bfloat16)], axis=1)
        home_values = jnp.concatenate([sink_values, value_vec.astype(jnp.bfloat16)], axis=1)
        home_scores = (
            jnp.einsum(
                "sthd,sjhd->sthj", query_halfwidth, home_keys, preferred_element_type=jnp.float32
            )
            * scale[None, None, :, None]
        )
        home_max = jnp.max(jnp.where(home_mask, home_scores, negative_big), axis=-1)
        home_weights = jnp.where(home_mask, jnp.exp(home_scores - home_max[..., None]), 0.0)
        home_sum = jnp.sum(home_weights, axis=-1)
        home_part = jnp.einsum(
            "sthj,sjhd->sthd",
            home_weights.astype(jnp.bfloat16),
            home_values,
            preferred_element_type=jnp.float32,
        )
        highest = jnp.maximum(home_max, jnp.max(part_max, axis=0))
        part_scale = jnp.exp(part_max - highest[None])
        home_scale = jnp.exp(home_max - highest)
        weight_sum = home_scale * home_sum + jnp.sum(part_scale * part_sum, axis=0)
        numerator = home_scale[..., None] * home_part + jnp.sum(
            part_scale[..., None] * part_numer, axis=0
        )
        attended = numerator / weight_sum[..., None]
        mixed_heads = (
            (rms_scale(readout, gain_head[None, None]) + attended)
            .astype(jnp.bfloat16)
            .reshape(rows, local_width)
        )
        partial_out = jnp.dot(mixed_heads, w_out[0], preferred_element_type=jnp.float32)
        mixer_out = head_sum(partial_out)
        stream_out = (stream.astype(jnp.float32) + mixer_out).astype(jnp.bfloat16)
        return stream_out, delta_state

    first_out, first_state = layer(embedded)
    received = lax.ppermute(first_out, "section", [(0, 1)])
    second_out, second_state = layer(received)
    is_first = section_index == 0
    produced = jnp.where(is_first, first_out, second_out).reshape(slot_count, token_count, width)
    final_state = jnp.where(is_first, first_state, second_state)
    return (produced[None], final_state[None])


def solution(mesh):
    return jax.shard_map(
        shards,
        mesh=mesh,
        in_specs=(
            P("req", None),
            P(),
            P(),
            P(("req", "head"), None),
            P("section", None, "req", None, "head"),
            P("section", None, "req", "head", None),
            P("section", "req", None, None, "head"),
            P("section", "req", None, None, "head"),
            P("section", None, None, "head"),
            P("section", "head", None),
            P("section", None, "head"),
            P("section", None, None, "head"),
            P("section", None),
            P("section", "head"),
            P("section", "head"),
        ),
        out_specs=(P("section", "req", None, None), P("section", "req", None, "head", None)),
        check_vma=False,
    )
```

```python
import jax
import jax.numpy as jnp
from jax import lax
from jax.experimental import pallas as pl
from jax.experimental.pallas import tpu as pltpu
from jax.sharding import PartitionSpec as P

WIN = 512


epsilon = 1e-06
negative_big = -1e30


def rms_scale(values, gain_row):
    return (
        values * lax.rsqrt(jnp.mean(values * values, axis=-1, keepdims=True) + epsilon) * gain_row
    )


def unit_rows(values):
    return values * lax.rsqrt(jnp.sum(values * values, axis=-1, keepdims=True) + epsilon)


def spread(value, axis):
    peers = lax.axis_size(axis)
    copies = jnp.broadcast_to(value[None], (peers,) + value.shape)
    return lax.all_to_all(copies, axis, 0, 0, tiled=True)


def head_sum(value):
    peers = lax.axis_size("head")
    step = 1
    while step < peers:
        pairs = [(i, i ^ step) for i in range(peers)]
        value = value + lax.ppermute(value, "head", pairs)
        step *= 2
    return value


def delta_rule_kernel(beta_ref, state_ref, key_ref, query_ref, value_ref, state_out, read_out):
    slots, key_rows, _ = state_ref.shape
    heads = key_ref.shape[1]
    tokens = value_ref.shape[1]
    def one_block(index, carry):
        s = index // heads
        h = index % heads
        cols = pl.ds(pl.multiple_of(h * key_rows, key_rows), key_rows)
        matrix = state_ref[s, :, cols]
        key_cols = key_ref[s, h]
        query_cols = query_ref[s, h]
        for t in range(tokens):
            k_t = key_cols[:, t : t + 1]
            predicted = jnp.sum(matrix * k_t, axis=0, keepdims=True)
            v_t = value_ref[s, pl.ds(t, 1), cols]
            gate = beta_ref[(s * tokens + t) * heads + h]
            matrix = matrix + gate * (k_t * (v_t - predicted))
            read_out[s, pl.ds(t, 1), cols] = jnp.sum(
                matrix * query_cols[:, t : t + 1], axis=0, keepdims=True
            )
        state_out[s, :, cols] = matrix
        return carry

    lax.fori_loop(0, slots * heads, one_block, 0)


def delta_rule(start_state, key_vec, query_vec, value_vec, beta_gate):
    slots, key_rows, heads, value_cols = start_state.shape
    tokens = key_vec.shape[1]
    vmem = pl.BlockSpec(memory_space=pltpu.VMEM)
    new_state, readout = pl.pallas_call(
        delta_rule_kernel,
        out_shape=(
            jax.ShapeDtypeStruct((slots, key_rows, heads * value_cols), jnp.float32),
            jax.ShapeDtypeStruct((slots, tokens, heads * value_cols), jnp.float32),
        ),
        in_specs=[pl.BlockSpec(memory_space=pltpu.SMEM), vmem, vmem, vmem, vmem],
        out_specs=(vmem, vmem),
        cost_estimate=pl.CostEstimate(
            flops=8 * slots * heads * tokens * key_rows * value_cols,
            bytes_accessed=8 * slots * key_rows * heads * value_cols,
            transcendentals=0,
        ),
    )(
        beta_gate.reshape(-1),
        start_state.reshape(slots, key_rows, heads * value_cols),
        jnp.transpose(key_vec, (0, 2, 3, 1)),
        jnp.transpose(query_vec, (0, 2, 3, 1)),
        value_vec.reshape(slots, tokens, heads * value_cols),
    )
    return (
        new_state.reshape(slots, key_rows, heads, value_cols),
        readout.reshape(slots, tokens, heads, value_cols),
    )


def shards(
    token_ids,
    request_order,
    window_lengths,
    embed_table,
    cache_arrived,
    state_arrived,
    conv_history,
    sink_cache,
    w_qkv,
    w_out,
    w_beta,
    conv_taps,
    pre_gain,
    out_gain,
    score_scale_table,
):
    slot_count, token_count = token_ids.shape
    groups = lax.axis_size("req")
    heads_dev = score_scale_table.shape[1]
    width = pre_gain.shape[1]
    local_width = out_gain.shape[1]
    head_dim = local_width // heads_dev
    group_index = lax.axis_index("req")
    section_index = lax.axis_index("section")
    vocab_dev = embed_table.shape[0]
    rows = slot_count * token_count

    all_ids = spread(token_ids, "req")
    first_row = lax.axis_index(("req", "head")) * vocab_dev
    onehot = (
        all_ids.reshape(-1)[:, None] == first_row + jnp.arange(vocab_dev, dtype=jnp.int32)[None, :]
    ).astype(jnp.bfloat16)
    looked_up = jnp.dot(onehot, embed_table, preferred_element_type=jnp.float32).astype(jnp.bfloat16)
    arrived_rows = lax.all_to_all(
        looked_up.reshape(groups, rows, width), "req", 0, 0, tiled=True
    )
    partial_rows = jnp.sum(arrived_rows.astype(jnp.float32), axis=0).astype(jnp.bfloat16)
    embedded = jnp.sum(spread(partial_rows, "head").astype(jnp.float32), axis=0).astype(jnp.bfloat16)

    ordered_states = jnp.take(state_arrived[0], request_order, axis=0)
    start_state = lax.all_to_all(ordered_states, "req", 0, 1, tiled=True)

    all_slots, cache_rows = cache_arrived.shape[1], cache_arrived.shape[2]
    by_head = jnp.transpose(
        cache_arrived[0].reshape(all_slots, cache_rows, 2, heads_dev, head_dim), (2, 0, 3, 1, 4)
    )
    ordered_cache = jnp.take(by_head, request_order, axis=1)
    stored_key_rows = ordered_cache[0]
    cache_values = ordered_cache[1]
    all_lengths = jnp.take(window_lengths, request_order)
    positions = group_index * cache_rows + jnp.arange(cache_rows, dtype=jnp.int32)
    new_index = jnp.arange(token_count, dtype=jnp.int32)
    cache_limit = jnp.maximum(WIN - all_lengths[:, None], new_index[None, :] + 1)
    cache_mask = positions[None, None, None, :] >= cache_limit[:, :, None, None]

    sink_count = sink_cache.shape[2]
    anchor_key_rows = sink_cache[0][:, :, 0].reshape(slot_count, sink_count, heads_dev, head_dim)
    sink_values = sink_cache[0][:, :, 1].reshape(slot_count, sink_count, heads_dev, head_dim)
    qkv_matrix = w_qkv[0].reshape(width, 3 * local_width)
    conv_weights = conv_taps[0]
    scale = score_scale_table[0]
    gain_head = out_gain[0].reshape(heads_dev, head_dim)
    history = conv_history[0]
    home_mask = jnp.concatenate(
        [
            jnp.ones((token_count, sink_count), jnp.bool_),
            new_index[None, :] <= new_index[:, None],
        ],
        axis=1,
    )[None, :, None, :]

    def layer(stream):
        normed = rms_scale(stream.astype(jnp.float32), pre_gain[0]).astype(jnp.bfloat16)
        projected = (
            jnp.dot(normed, qkv_matrix, preferred_element_type=jnp.float32)
            .astype(jnp.bfloat16)
            .reshape(slot_count, token_count, 3, local_width)
        )
        sequence = jnp.concatenate([history, projected], axis=1).astype(jnp.float32)
        taps = conv_weights.shape[0]
        mixed_rows = sum(
            sequence[:, i : i + token_count] * conv_weights[i][None, None] for i in range(taps)
        )
        activated = jax.nn.silu(mixed_rows)
        query_vec = unit_rows(activated[:, :, 0].reshape(slot_count, token_count, heads_dev, head_dim))
        key_vec = unit_rows(activated[:, :, 1].reshape(slot_count, token_count, heads_dev, head_dim))
        value_vec = activated[:, :, 2].reshape(slot_count, token_count, heads_dev, head_dim)
        beta_gate = jax.nn.sigmoid(
            jnp.dot(normed, w_beta[0], preferred_element_type=jnp.float32)
        ).reshape(slot_count, token_count, heads_dev)

        query_halfwidth = query_vec.astype(jnp.bfloat16)
        all_queries = spread(query_halfwidth, "req").reshape(
            all_slots, token_count, heads_dev, head_dim
        )
        stored_scores = (
            jnp.einsum(
                "rthd,rhwd->rthw",
                all_queries,
                stored_key_rows,
                preferred_element_type=jnp.float32,
            )
            * scale[None, None, :, None]
        )
        local_max = jnp.max(jnp.where(cache_mask, stored_scores, negative_big), axis=-1)
        local_weights = jnp.where(cache_mask, jnp.exp(stored_scores - local_max[..., None]), 0.0)
        local_sum = jnp.sum(local_weights, axis=-1)
        local_part = jnp.einsum(
            "rthw,rhwd->rthd",
            local_weights.astype(jnp.bfloat16),
            cache_values,
            preferred_element_type=jnp.float32,
        )
        stats_count = 2 * token_count * heads_dev
        stats = jnp.concatenate(
            [
                jnp.concatenate([local_sum, local_max], axis=-1).reshape(all_slots, stats_count),
                jnp.zeros((all_slots, head_dim - stats_count), jnp.float32),
            ],
            axis=-1,
        )
        packed = jnp.concatenate(
            [
                local_part.reshape(all_slots, token_count * heads_dev, head_dim),
                stats[:, None, :],
            ],
            axis=1,
        ).reshape(groups, slot_count, token_count * heads_dev + 1, head_dim)
        gathered = lax.all_to_all(packed, "req", 0, 0, tiled=True)
        part_numer = gathered[:, :, : token_count * heads_dev].reshape(
            groups, slot_count, token_count, heads_dev, head_dim
        )
        part_stats = gathered[:, :, token_count * heads_dev, :stats_count].reshape(
            groups, slot_count, token_count, 2 * heads_dev
        )
        part_sum = part_stats[..., :heads_dev]
        part_max = part_stats[..., heads_dev:]

        delta_state, readout = delta_rule(start_state, key_vec, query_vec, value_vec, beta_gate)

        home_keys = jnp.concatenate([anchor_key_rows, key_vec.astype(jnp.bfloat16)], axis=1)
        home_values = jnp.concatenate([sink_values, value_vec.astype(jnp.bfloat16)], axis=1)
        home_scores = (
            jnp.einsum(
                "sthd,sjhd->sthj", query_halfwidth, home_keys, preferred_element_type=jnp.float32
            )
            * scale[None, None, :, None]
        )
        home_max = jnp.max(jnp.where(home_mask, home_scores, negative_big), axis=-1)
        home_weights = jnp.where(home_mask, jnp.exp(home_scores - home_max[..., None]), 0.0)
        home_sum = jnp.sum(home_weights, axis=-1)
        home_part = jnp.einsum(
            "sthj,sjhd->sthd",
            home_weights.astype(jnp.bfloat16),
            home_values,
            preferred_element_type=jnp.float32,
        )
        highest = jnp.maximum(home_max, jnp.max(part_max, axis=0))
        part_scale = jnp.exp(part_max - highest[None])
        home_scale = jnp.exp(home_max - highest)
        weight_sum = home_scale * home_sum + jnp.sum(part_scale * part_sum, axis=0)
        numerator = home_scale[..., None] * home_part + jnp.sum(
            part_scale[..., None] * part_numer, axis=0
        )
        attended = numerator / weight_sum[..., None]
        mixed_heads = (
            (rms_scale(readout, gain_head[None, None]) + attended)
            .astype(jnp.bfloat16)
            .reshape(rows, local_width)
        )
        partial_out = jnp.dot(mixed_heads, w_out[0], preferred_element_type=jnp.float32)
        mixer_out = head_sum(partial_out)
        stream_out = (stream.astype(jnp.float32) + mixer_out).astype(jnp.bfloat16)
        return stream_out, delta_state

    first_out, first_state = layer(embedded)
    received = lax.ppermute(first_out, "section", [(0, 1)])
    second_out, second_state = layer(received)
    is_first = section_index == 0
    produced = jnp.where(is_first, first_out, second_out).reshape(slot_count, token_count, width)
    final_state = jnp.where(is_first, first_state, second_state)
    return (produced[None], final_state[None])


def solution(mesh):
    return jax.shard_map(
        shards,
        mesh=mesh,
        in_specs=(
            P("req", None),
            P(),
            P(),
            P(("req", "head"), None),
            P("section", None, "req", None, "head"),
            P("section", None, "req", "head", None),
            P("section", "req", None, None, "head"),
            P("section", "req", None, None, "head"),
            P("section", None, None, "head"),
            P("section", "head", None),
            P("section", None, "head"),
            P("section", None, None, "head"),
            P("section", None),
            P("section", "head"),
            P("section", "head"),
        ),
        out_specs=(P("section", "req", None, None), P("section", "req", None, "head", None)),
        check_vma=False,
    )
```

```python
import jax
import jax.numpy as jnp
from jax import lax
from jax.experimental import pallas as pl
from jax.experimental.pallas import tpu as pltpu
from jax.sharding import PartitionSpec as P

WIN = 512


epsilon = 1e-06
negative_big = -1e30


def rms_scale(values, gain_row):
    return (
        values * lax.rsqrt(jnp.mean(values * values, axis=-1, keepdims=True) + epsilon) * gain_row
    )


def unit_rows(values):
    return values * lax.rsqrt(jnp.sum(values * values, axis=-1, keepdims=True) + epsilon)


def spread(value, axis):
    peers = lax.axis_size(axis)
    copies = jnp.broadcast_to(value[None], (peers,) + value.shape)
    return lax.all_to_all(copies, axis, 0, 0, tiled=True)


def head_sum(value):
    peers = lax.axis_size("head")
    if peers == 4:
        first = [(i, i ^ 1) for i in range(peers)]
        second = [(i, (i + 1) % peers if i % 2 else (i - 1) % peers) for i in range(peers)]
        value = value + lax.ppermute(value, "head", first)
        return value + lax.ppermute(value, "head", second)
    step = 1
    while step < peers:
        pairs = [(i, i ^ step) for i in range(peers)]
        value = value + lax.ppermute(value, "head", pairs)
        step *= 2
    return value


def delta_rule_kernel(beta_ref, state_ref, key_ref, query_ref, value_ref, state_out, read_out):
    slots, key_rows, _ = state_ref.shape
    heads = key_ref.shape[1]
    tokens = value_ref.shape[1]
    def one_block(index, carry):
        s = index // heads
        h = index % heads
        cols = pl.ds(pl.multiple_of(h * key_rows, key_rows), key_rows)
        matrix = state_ref[s, :, cols]
        key_cols = key_ref[s, h]
        query_cols = query_ref[s, h]
        for t in range(tokens):
            k_t = key_cols[:, t : t + 1]
            predicted = jnp.sum(matrix * k_t, axis=0, keepdims=True)
            v_t = value_ref[s, pl.ds(t, 1), cols]
            gate = beta_ref[(s * tokens + t) * heads + h]
            matrix = matrix + gate * (k_t * (v_t - predicted))
            read_out[s, pl.ds(t, 1), cols] = jnp.sum(
                matrix * query_cols[:, t : t + 1], axis=0, keepdims=True
            )
        state_out[s, :, cols] = matrix
        return carry

    lax.fori_loop(0, slots * heads, one_block, 0)


def delta_rule(start_state, key_vec, query_vec, value_vec, beta_gate):
    slots, key_rows, heads, value_cols = start_state.shape
    tokens = key_vec.shape[1]
    vmem = pl.BlockSpec(memory_space=pltpu.VMEM)
    new_state, readout = pl.pallas_call(
        delta_rule_kernel,
        out_shape=(
            jax.ShapeDtypeStruct((slots, key_rows, heads * value_cols), jnp.float32),
            jax.ShapeDtypeStruct((slots, tokens, heads * value_cols), jnp.float32),
        ),
        in_specs=[pl.BlockSpec(memory_space=pltpu.SMEM), vmem, vmem, vmem, vmem],
        out_specs=(vmem, vmem),
        cost_estimate=pl.CostEstimate(
            flops=8 * slots * heads * tokens * key_rows * value_cols,
            bytes_accessed=8 * slots * key_rows * heads * value_cols,
            transcendentals=0,
        ),
    )(
        beta_gate.reshape(-1),
        start_state.reshape(slots, key_rows, heads * value_cols),
        jnp.transpose(key_vec, (0, 2, 3, 1)),
        jnp.transpose(query_vec, (0, 2, 3, 1)),
        value_vec.reshape(slots, tokens, heads * value_cols),
    )
    return (
        new_state.reshape(slots, key_rows, heads, value_cols),
        readout.reshape(slots, tokens, heads, value_cols),
    )


def shards(
    token_ids,
    request_order,
    window_lengths,
    embed_table,
    cache_arrived,
    state_arrived,
    conv_history,
    sink_cache,
    w_qkv,
    w_out,
    w_beta,
    conv_taps,
    pre_gain,
    out_gain,
    score_scale_table,
):
    slot_count, token_count = token_ids.shape
    groups = lax.axis_size("req")
    heads_dev = score_scale_table.shape[1]
    width = pre_gain.shape[1]
    local_width = out_gain.shape[1]
    head_dim = local_width // heads_dev
    group_index = lax.axis_index("req")
    section_index = lax.axis_index("section")
    vocab_dev = embed_table.shape[0]
    rows = slot_count * token_count

    all_ids = spread(token_ids, "req")
    first_row = lax.axis_index(("req", "head")) * vocab_dev
    onehot = (
        all_ids.reshape(-1)[:, None] == first_row + jnp.arange(vocab_dev, dtype=jnp.int32)[None, :]
    ).astype(jnp.bfloat16)
    looked_up = jnp.dot(onehot, embed_table, preferred_element_type=jnp.float32).astype(jnp.bfloat16)
    arrived_rows = lax.all_to_all(
        looked_up.reshape(groups, rows, width), "req", 0, 0, tiled=True
    )
    partial_rows = jnp.sum(arrived_rows.astype(jnp.float32), axis=0).astype(jnp.bfloat16)
    embedded = jnp.sum(spread(partial_rows, "head").astype(jnp.float32), axis=0).astype(jnp.bfloat16)

    ordered_states = jnp.take(state_arrived[0], request_order, axis=0)
    start_state = lax.all_to_all(ordered_states, "req", 0, 1, tiled=True)

    all_slots, cache_rows = cache_arrived.shape[1], cache_arrived.shape[2]
    by_head = jnp.transpose(
        cache_arrived[0].reshape(all_slots, cache_rows, 2, heads_dev, head_dim), (2, 0, 3, 1, 4)
    )
    ordered_cache = jnp.take(by_head, request_order, axis=1)
    stored_key_rows = ordered_cache[0]
    cache_values = ordered_cache[1]
    all_lengths = jnp.take(window_lengths, request_order)
    positions = group_index * cache_rows + jnp.arange(cache_rows, dtype=jnp.int32)
    new_index = jnp.arange(token_count, dtype=jnp.int32)
    cache_limit = jnp.maximum(WIN - all_lengths[:, None], new_index[None, :] + 1)
    cache_mask = positions[None, None, None, :] >= cache_limit[:, :, None, None]

    sink_count = sink_cache.shape[2]
    anchor_key_rows = sink_cache[0][:, :, 0].reshape(slot_count, sink_count, heads_dev, head_dim)
    sink_values = sink_cache[0][:, :, 1].reshape(slot_count, sink_count, heads_dev, head_dim)
    qkv_matrix = w_qkv[0].reshape(width, 3 * local_width)
    conv_weights = conv_taps[0]
    scale = score_scale_table[0]
    gain_head = out_gain[0].reshape(heads_dev, head_dim)
    history = conv_history[0]
    home_mask = jnp.concatenate(
        [
            jnp.ones((token_count, sink_count), jnp.bool_),
            new_index[None, :] <= new_index[:, None],
        ],
        axis=1,
    )[None, :, None, :]

    def layer(stream):
        normed = rms_scale(stream.astype(jnp.float32), pre_gain[0]).astype(jnp.bfloat16)
        projected = (
            jnp.dot(normed, qkv_matrix, preferred_element_type=jnp.float32)
            .astype(jnp.bfloat16)
            .reshape(slot_count, token_count, 3, local_width)
        )
        sequence = jnp.concatenate([history, projected], axis=1).astype(jnp.float32)
        taps = conv_weights.shape[0]
        mixed_rows = sum(
            sequence[:, i : i + token_count] * conv_weights[i][None, None] for i in range(taps)
        )
        activated = jax.nn.silu(mixed_rows)
        query_vec = unit_rows(activated[:, :, 0].reshape(slot_count, token_count, heads_dev, head_dim))
        key_vec = unit_rows(activated[:, :, 1].reshape(slot_count, token_count, heads_dev, head_dim))
        value_vec = activated[:, :, 2].reshape(slot_count, token_count, heads_dev, head_dim)
        beta_gate = jax.nn.sigmoid(
            jnp.dot(normed, w_beta[0], preferred_element_type=jnp.float32)
        ).reshape(slot_count, token_count, heads_dev)

        query_halfwidth = query_vec.astype(jnp.bfloat16)
        all_queries = spread(query_halfwidth, "req").reshape(
            all_slots, token_count, heads_dev, head_dim
        )
        stored_scores = (
            jnp.einsum(
                "rthd,rhwd->rthw",
                all_queries,
                stored_key_rows,
                preferred_element_type=jnp.float32,
            )
            * scale[None, None, :, None]
        )
        local_max = jnp.max(jnp.where(cache_mask, stored_scores, negative_big), axis=-1)
        local_weights = jnp.where(cache_mask, jnp.exp(stored_scores - local_max[..., None]), 0.0)
        local_sum = jnp.sum(local_weights, axis=-1)
        local_part = jnp.einsum(
            "rthw,rhwd->rthd",
            local_weights.astype(jnp.bfloat16),
            cache_values,
            preferred_element_type=jnp.float32,
        )
        stats_count = 2 * token_count * heads_dev
        stats = jnp.concatenate(
            [
                jnp.concatenate([local_sum, local_max], axis=-1).reshape(all_slots, stats_count),
                jnp.zeros((all_slots, head_dim - stats_count), jnp.float32),
            ],
            axis=-1,
        )
        packed = jnp.concatenate(
            [
                local_part.reshape(all_slots, token_count * heads_dev, head_dim),
                stats[:, None, :],
            ],
            axis=1,
        ).reshape(groups, slot_count, token_count * heads_dev + 1, head_dim)
        gathered = lax.all_to_all(packed, "req", 0, 0, tiled=True)
        part_numer = gathered[:, :, : token_count * heads_dev].reshape(
            groups, slot_count, token_count, heads_dev, head_dim
        )
        part_stats = gathered[:, :, token_count * heads_dev, :stats_count].reshape(
            groups, slot_count, token_count, 2 * heads_dev
        )
        part_sum = part_stats[..., :heads_dev]
        part_max = part_stats[..., heads_dev:]

        delta_state, readout = delta_rule(start_state, key_vec, query_vec, value_vec, beta_gate)

        home_keys = jnp.concatenate([anchor_key_rows, key_vec.astype(jnp.bfloat16)], axis=1)
        home_values = jnp.concatenate([sink_values, value_vec.astype(jnp.bfloat16)], axis=1)
        home_scores = (
            jnp.einsum(
                "sthd,sjhd->sthj", query_halfwidth, home_keys, preferred_element_type=jnp.float32
            )
            * scale[None, None, :, None]
        )
        home_max = jnp.max(jnp.where(home_mask, home_scores, negative_big), axis=-1)
        home_weights = jnp.where(home_mask, jnp.exp(home_scores - home_max[..., None]), 0.0)
        home_sum = jnp.sum(home_weights, axis=-1)
        home_part = jnp.einsum(
            "sthj,sjhd->sthd",
            home_weights.astype(jnp.bfloat16),
            home_values,
            preferred_element_type=jnp.float32,
        )
        highest = jnp.maximum(home_max, jnp.max(part_max, axis=0))
        part_scale = jnp.exp(part_max - highest[None])
        home_scale = jnp.exp(home_max - highest)
        weight_sum = home_scale * home_sum + jnp.sum(part_scale * part_sum, axis=0)
        numerator = home_scale[..., None] * home_part + jnp.sum(
            part_scale[..., None] * part_numer, axis=0
        )
        attended = numerator / weight_sum[..., None]
        mixed_heads = (
            (rms_scale(readout, gain_head[None, None]) + attended)
            .astype(jnp.bfloat16)
            .reshape(rows, local_width)
        )
        partial_out = jnp.dot(mixed_heads, w_out[0], preferred_element_type=jnp.float32)
        mixer_out = head_sum(partial_out)
        stream_out = (stream.astype(jnp.float32) + mixer_out).astype(jnp.bfloat16)
        return stream_out, delta_state

    first_out, first_state = layer(embedded)
    received = lax.ppermute(first_out, "section", [(0, 1)])
    second_out, second_state = layer(received)
    is_first = section_index == 0
    produced = jnp.where(is_first, first_out, second_out).reshape(slot_count, token_count, width)
    final_state = jnp.where(is_first, first_state, second_state)
    return (produced[None], final_state[None])


def solution(mesh):
    return jax.shard_map(
        shards,
        mesh=mesh,
        in_specs=(
            P("req", None),
            P(),
            P(),
            P(("req", "head"), None),
            P("section", None, "req", None, "head"),
            P("section", None, "req", "head", None),
            P("section", "req", None, None, "head"),
            P("section", "req", None, None, "head"),
            P("section", None, None, "head"),
            P("section", "head", None),
            P("section", None, "head"),
            P("section", None, None, "head"),
            P("section", None),
            P("section", "head"),
            P("section", "head"),
        ),
        out_specs=(P("section", "req", None, None), P("section", "req", None, "head", None)),
        check_vma=False,
    )
```
